32 devices in a mesh: space: 16 (over z, x, core), tm: 2 (over y).
Axes of the slice: x: 2, y: 2, z: 4, core: 2. Of those that a mesh axis runs over, the one named last changes fastest.
Arguments:
- guess_pressure: float32 [2, 32, 64, 128], P('tm', 'space'), may hold values from -6 to 6
- guess_velocity: float32 [2, 3, 32, 64, 128], P('tm', None, 'space'), may hold values from -6 to 6
- initial_pressure: float32 [32, 64, 128], P('space'), may hold values from -6 to 6
- initial_velocity: float32 [3, 32, 64, 128], P(None, 'space'), may hold values from -6 to 6
- stiffness: float32 [32, 64, 128], P('space'), may hold values from 0.5 to 2
- inv_mass: float32 [32, 64, 128], P('space'), may hold values from 0.5 to 2
Outputs:
- corrected_pressure: float32 [2, 32, 64, 128], P('tm', 'space')
- corrected_velocity: float32 [2, 3, 32, 64, 128], P('tm', None, 'space')
- residual_pressure: float32 [2, 32, 64, 128], P('tm', 'space')
- residual_velocity: float32 [2, 3, 32, 64, 128], P('tm', None, 'space')
The draws below stay inside these ranges and needn't reach their ends.
All inputs are finite; a program needn't handle non-finite values.
Results may differ from the reference program's by a relative error of at most 0.00002.
Values sent between devices are 32-bit elements; how exact they have to be, the bound alone decides.
No kernel may reach another device: no remote copies, remote signals or barrier semaphores. Data moves between devices by JAX's collectives and lax.ppermute only.
A program may use at most 64 MiB of HBM per device.

```python
import math
import jax
import jax.numpy as jnp

NY = 64
NZ = 128
STEPS = 4
NX = 32
N_TM = 2


def steps_of(stream_key, dims, pieces, least, top_value):
    loudness, own = 1.0, jax.random.fold_in(stream_key, 6)
    for position, blocks in pieces:
        heights = jnp.exp(jax.random.uniform(jax.random.fold_in(own, position), (blocks,), jnp.float32, least / len(pieces), top_value / len(pieces)))
        loudness = loudness * jnp.repeat(heights, dims[position] // blocks).reshape([-1 if axis == position else 1 for axis in range(len(dims))])
    return loudness


def bell_draw(stream_key, dims, deviation, limit, cuts=(), dtype=jnp.bfloat16):
    factor_of = steps_of(stream_key, dims, cuts, -0.22, 0.18) if cuts else 1.0
    values = jax.random.normal(stream_key, dims, jnp.float32) * deviation * factor_of
    return jnp.minimum(jnp.maximum(values, -limit), limit).astype(dtype)


def setup_inputs(seed: int = 0) -> dict:
    splits = jax.random.split(jax.random.key(seed), 7)
    return {
        "guess_pressure": bell_draw(splits[0], (N_TM, NX, NY, NZ), 1.0, 6.0, ((0, 2), (1, 16)), jnp.float32),
        "guess_velocity": bell_draw(splits[1], (N_TM, 3, NX, NY, NZ), 1.0, 6.0, ((0, 2), (2, 16)), jnp.float32),
        "initial_pressure": bell_draw(splits[2], (NX, NY, NZ), 1.0, 6.0, ((0, 16),), jnp.float32),
        "initial_velocity": bell_draw(splits[3], (3, NX, NY, NZ), 1.0, 6.0, ((1, 16),), jnp.float32),
        "stiffness": jnp.clip(jnp.exp(math.log(2.0) - 1.3862944 * jax.random.uniform(splits[4], (NX, NY, NZ), jnp.float32) ** steps_of(splits[4], (NX, NY, NZ), ((0, 16),), -0.2, 0.2)), 0.5, 2.0),
        "inv_mass": jnp.clip(jnp.exp(math.log(2.0) - 1.3862944 * jax.random.uniform(splits[5], (NX, NY, NZ), jnp.float32) ** steps_of(splits[5], (NX, NY, NZ), ((0, 16),), -0.2, 0.2)), 0.5, 2.0),
    }


DT_COARSE = 0.4


def neighbour_sum(values, offset, axis):
    return values + jnp.roll(values, offset, axis=axis)


def node_forces(pressure, lower_zones):
    combined = pressure + lower_zones
    force_x = 0.25 * (neighbour_sum(neighbour_sum(lower_zones, 1, -1), 1, -2) - neighbour_sum(neighbour_sum(pressure, 1, -1), 1, -2))
    across_z = neighbour_sum(combined, 1, -1)
    force_y = 0.25 * (jnp.roll(across_z, 1, axis=-2) - across_z)
    across_y = neighbour_sum(combined, 1, -2)
    force_z = 0.25 * (jnp.roll(across_y, 1, axis=-1) - across_y)
    return jnp.stack([force_x, force_y, force_z])


def zone_divergence(velocity, upper_nodes):
    diff_x = neighbour_sum(neighbour_sum(upper_nodes[0] - velocity[0], -1, -1), -1, -2)
    sum_y = neighbour_sum(velocity[1] + upper_nodes[1], -1, -1)
    diff_y = jnp.roll(sum_y, -1, axis=-2) - sum_y
    sum_z = neighbour_sum(velocity[2] + upper_nodes[2], -1, -2)
    diff_z = jnp.roll(sum_z, -1, axis=-1) - sum_z
    return 0.25 * (diff_x + diff_y + diff_z)


def advance(pressure, velocity, stiffness, inv_mass, step_size):
    empty_plane = jnp.zeros_like(pressure[:1])
    lower_zones = jnp.concatenate([empty_plane, pressure[:-1]], axis=0)
    forces = node_forces(pressure, lower_zones)
    velocity = velocity + step_size * inv_mass * forces
    upper_nodes = jnp.concatenate([velocity[:, 1:], jnp.zeros_like(velocity[:, :1])], axis=1)
    pressure = pressure - step_size * stiffness * zone_divergence(velocity, upper_nodes)
    return pressure, velocity


def propagate(pressure, velocity, stiffness, inv_mass):
    fine_size = DT_COARSE / STEPS
    for repeat in range(STEPS):
        pressure, velocity = advance(pressure, velocity, stiffness, inv_mass, fine_size)
    return pressure, velocity


def reference(guess_pressure, guess_velocity, initial_pressure, initial_velocity, stiffness, inv_mass):
    relaxed = []
    for group in range(N_TM):
        relaxed.append(propagate(guess_pressure[group], guess_velocity[group], stiffness, inv_mass))
    corrected_p = []
    corrected_v = []
    residual_p = []
    residual_v = []
    error_p = None
    error_v = None
    for group in range(N_TM):
        if group == 0:
            start_p, start_v = initial_pressure, initial_velocity
        else:
            start_p, start_v = relaxed[group - 1]
        end_p, end_v = propagate(start_p, start_v, stiffness, inv_mass)
        resid_p = end_p - relaxed[group][0]
        resid_v = end_v - relaxed[group][1]
        if group == 0:
            error_p, error_v = resid_p, resid_v
        else:
            moved_p, moved_v = advance(error_p, error_v, stiffness, inv_mass, DT_COARSE)
            error_p = resid_p + moved_p
            error_v = resid_v + moved_v
        corrected_p.append(relaxed[group][0] + error_p)
        corrected_v.append(relaxed[group][1] + error_v)
        residual_p.append(resid_p)
        residual_v.append(resid_v)
    return (jnp.stack(corrected_p), jnp.stack(corrected_v), jnp.stack(residual_p), jnp.stack(residual_v))
```

```python
import jax
import jax.numpy as jnp
from jax import lax
from jax.sharding import PartitionSpec as P

STEPS = 4


DT_COARSE = 0.4


def from_behind(x, axis, by):
    size = lax.axis_size(axis)
    pairs = [(i, i + by) for i in range(size) if 0 <= i + by < size]
    return lax.ppermute(x, axis, pairs)


def neighbour_sum(values, offset, axis):
    return values + jnp.roll(values, offset, axis=axis)


def node_forces(pressure, lower_zones):
    combined = pressure + lower_zones
    force_x = 0.25 * (
        neighbour_sum(neighbour_sum(lower_zones, 1, -1), 1, -2)
        - neighbour_sum(neighbour_sum(pressure, 1, -1), 1, -2)
    )
    across_z = neighbour_sum(combined, 1, -1)
    force_y = 0.25 * (jnp.roll(across_z, 1, axis=-2) - across_z)
    across_y = neighbour_sum(combined, 1, -2)
    force_z = 0.25 * (jnp.roll(across_y, 1, axis=-1) - across_y)
    return jnp.stack([force_x, force_y, force_z], axis=-4)


def zone_divergence(velocity, upper_nodes):
    v0, v1, v2 = velocity[..., 0, :, :, :], velocity[..., 1, :, :, :], velocity[..., 2, :, :, :]
    u0, u1, u2 = upper_nodes[..., 0, :, :, :], upper_nodes[..., 1, :, :, :], upper_nodes[..., 2, :, :, :]
    diff_x = neighbour_sum(neighbour_sum(u0 - v0, -1, -1), -1, -2)
    sum_y = neighbour_sum(v1 + u1, -1, -1)
    diff_y = jnp.roll(sum_y, -1, axis=-2) - sum_y
    sum_z = neighbour_sum(v2 + u2, -1, -2)
    diff_z = jnp.roll(sum_z, -1, axis=-1) - sum_z
    return 0.25 * (diff_x + diff_y + diff_z)


def window_step(pressure, velocity, stiffness, inv_mass, step_size):
    forces = node_forces(pressure[..., 1:, :, :], pressure[..., :-1, :, :])
    velocity = velocity + step_size * inv_mass * forces
    pressure = pressure[..., 1:-1, :, :] - step_size * stiffness * zone_divergence(
        velocity[..., :-1, :, :], velocity[..., 1:, :, :]
    )
    return pressure, velocity


def window_propagate(pressure, velocity, stiffness, inv_mass, steps, step_size):
    for j in range(steps):
        width = pressure.shape[-3]
        pressure, velocity = window_step(
            pressure, velocity, stiffness[j : j + width - 2], inv_mass[j : j + width - 1], step_size
        )
        if j + 1 < steps:
            velocity = velocity[..., 1:-1, :, :]
    n = pressure.shape[-3]
    return pressure, velocity[..., :n, :, :]


def halo(blocks, widths):
    n = blocks[0].shape[1]
    reach = [-(-w // n) for w in widths]
    lefts = [[] for _ in blocks]
    rights = [[] for _ in blocks]
    for d in range(1, max(reach) + 1):
        chosen = [i for i, q in enumerate(reach) if q >= d]
        sizes = [blocks[i].shape[0] for i in chosen]
        packed = jnp.concatenate([blocks[i] for i in chosen], axis=0)
        from_left = from_behind(packed, "space", d)
        from_right = from_behind(packed, "space", -d)
        offset = 0
        for i, s in zip(chosen, sizes):
            lefts[i].insert(0, from_left[offset : offset + s])
            rights[i].append(from_right[offset : offset + s])
            offset += s
    out = []
    for i, b in enumerate(blocks):
        ext = jnp.concatenate(lefts[i] + [b] + rights[i], axis=1)
        start = reach[i] * n - widths[i]
        out.append(ext[:, start : start + n + 2 * widths[i]])
    return out


def on_device(
    guess_pressure, guess_velocity, initial_pressure, initial_velocity, stiffness, inv_mass
):
    fine_size = DT_COARSE / STEPS
    n = stiffness.shape[0]
    groups = lax.axis_size("tm")
    group = lax.axis_index("tm")

    state = jnp.concatenate(
        [
            guess_pressure[0][None],
            initial_pressure[None],
            guess_velocity[0],
            initial_velocity,
            stiffness[None],
            inv_mass[None],
        ],
        axis=0,
    )
    (ext,) = halo([state], [STEPS])
    ext_p = ext[0:2]
    ext_v = ext[2:8, 1:].reshape(2, 3, n + 2 * STEPS - 1, *ext.shape[2:])
    ext_k = ext[8, 1:-1]
    ext_m = ext[9, 1:]
    first_p, first_v = window_propagate(ext_p, ext_v, ext_k, ext_m, STEPS, fine_size)
    relaxed_p, relaxed_v = first_p[0], first_v[0]
    own_end_p, own_end_v = first_p[1], first_v[1]
    early_p = own_end_p - relaxed_p
    early_v = own_end_v - relaxed_v

    sent = jnp.concatenate([relaxed_p[None], relaxed_v, early_p[None], early_v], axis=0)
    got = from_behind(sent, "tm", 1)
    got_relaxed, got_resid = halo([got[0:4], got[4:8]], [STEPS, 1])

    late_p, late_v = window_propagate(
        got_relaxed[0],
        got_relaxed[1:4, 1:],
        ext_k,
        ext_m,
        STEPS,
        fine_size,
    )
    first_group = group == 0
    end_p = jnp.where(first_group, own_end_p, late_p)
    end_v = jnp.where(first_group, own_end_v, late_v)
    resid_p = end_p - relaxed_p
    resid_v = end_v - relaxed_v

    coarse_k = ext_k[STEPS - 1 : STEPS - 1 + n]
    coarse_m = ext_m[STEPS - 1 : STEPS - 1 + n + 1]
    if groups == 2:
        moved_p, moved_v = window_propagate(
            got_resid[0], got_resid[1:4, 1:], coarse_k, coarse_m, 1, DT_COARSE
        )
        error_p = resid_p + moved_p
        error_v = resid_v + moved_v
    else:
        error_p, error_v = resid_p, resid_v
        carried_p, carried_v = resid_p, resid_v
        for repeat in range(groups - 1):
            carried = from_behind(
                jnp.concatenate([carried_p[None], carried_v], axis=0), "tm", 1
            )
            (carried,) = halo([carried], [1])
            carried_p, carried_v = window_propagate(
                carried[0], carried[1:4, 1:], coarse_k, coarse_m, 1, DT_COARSE
            )
            error_p = error_p + carried_p
            error_v = error_v + carried_v
    corrected_p = relaxed_p + error_p
    corrected_v = relaxed_v + error_v
    return (corrected_p[None], corrected_v[None], resid_p[None], resid_v[None])


def solution(mesh):
    placed = (
        P("tm", "space", None, None),
        P("tm", None, "space", None, None),
        P("space", None, None),
        P(None, "space", None, None),
        P("space", None, None),
        P("space", None, None),
    )
    return jax.shard_map(
        on_device,
        mesh=mesh,
        in_specs=placed,
        out_specs=(
            P("tm", "space", None, None),
            P("tm", None, "space", None, None),
            P("tm", "space", None, None),
            P("tm", None, "space", None, None),
        ),
        check_vma=False,
    )
```

```python
import jax
import jax.numpy as jnp
from jax import lax
from jax.sharding import PartitionSpec as P

STEPS = 4


DT_COARSE = 0.4


def from_behind(x, axis, by):
    size = lax.axis_size(axis)
    pairs = [(i, i + by) for i in range(size) if 0 <= i + by < size]
    return lax.ppermute(x, axis, pairs)


def neighbour_sum(values, offset, axis):
    return values + jnp.roll(values, offset, axis=axis)


def node_forces(pressure, lower_zones):
    combined = pressure + lower_zones
    force_x = 0.25 * (
        neighbour_sum(neighbour_sum(lower_zones, 1, -1), 1, -2)
        - neighbour_sum(neighbour_sum(pressure, 1, -1), 1, -2)
    )
    across_z = neighbour_sum(combined, 1, -1)
    force_y = 0.25 * (jnp.roll(across_z, 1, axis=-2) - across_z)
    across_y = neighbour_sum(combined, 1, -2)
    force_z = 0.25 * (jnp.roll(across_y, 1, axis=-1) - across_y)
    return jnp.stack([force_x, force_y, force_z], axis=-4)


def parts(velocity):
    return velocity[..., 0, :, :, :], velocity[..., 1, :, :, :], velocity[..., 2, :, :, :]


def zone_divergence(velocity, upper_nodes):
    v0, v1, v2 = parts(velocity)
    u0, u1, u2 = parts(upper_nodes)
    diff_x = neighbour_sum(neighbour_sum(u0 - v0, -1, -1), -1, -2)
    sum_y = neighbour_sum(v1 + u1, -1, -1)
    diff_y = jnp.roll(sum_y, -1, axis=-2) - sum_y
    sum_z = neighbour_sum(v2 + u2, -1, -2)
    diff_z = jnp.roll(sum_z, -1, axis=-1) - sum_z
    return 0.25 * (diff_x + diff_y + diff_z)


def upper_part(upper_nodes):
    u0, u1, u2 = parts(upper_nodes)
    diff_x = neighbour_sum(neighbour_sum(u0, -1, -1), -1, -2)
    sum_y = neighbour_sum(u1, -1, -1)
    diff_y = jnp.roll(sum_y, -1, axis=-2) - sum_y
    sum_z = neighbour_sum(u2, -1, -2)
    diff_z = jnp.roll(sum_z, -1, axis=-1) - sum_z
    return diff_x + diff_y + diff_z


def lower_part(velocity):
    v0, v1, v2 = parts(velocity)
    diff_x = neighbour_sum(neighbour_sum(-v0, -1, -1), -1, -2)
    sum_y = neighbour_sum(v1, -1, -1)
    diff_y = jnp.roll(sum_y, -1, axis=-2) - sum_y
    sum_z = neighbour_sum(v2, -1, -2)
    diff_z = jnp.roll(sum_z, -1, axis=-1) - sum_z
    return diff_x + diff_y + diff_z


def advance(pressure, velocity, stiffness, inv_mass, next_mass, step_size):
    first = pressure[..., :1, :, :]
    last = pressure[..., -1:, :, :]
    empty = jnp.zeros_like(first)
    partial = velocity[..., :1, :, :] + step_size * inv_mass[:1] * node_forces(first, empty)
    from_left = from_behind(last, "space", 1)
    from_right = from_behind(upper_part(partial), "space", -1)
    lower_zones = jnp.concatenate([from_left, pressure[..., :-1, :, :]], axis=-3)
    forces = node_forces(pressure, lower_zones)
    velocity = velocity + step_size * inv_mass * forces
    inner = zone_divergence(velocity[..., :-1, :, :], velocity[..., 1:, :, :])
    own_share = upper_part(step_size * next_mass * node_forces(empty, last))
    edge = 0.25 * (lower_part(velocity[..., -1:, :, :]) + (from_right + own_share))
    div = jnp.concatenate([inner, edge], axis=-3)
    pressure = pressure - step_size * stiffness * div
    return pressure, velocity


def propagate(pressure, velocity, stiffness, inv_mass, next_mass):
    fine_size = DT_COARSE / STEPS
    for repeat in range(STEPS):
        pressure, velocity = advance(pressure, velocity, stiffness, inv_mass, next_mass, fine_size)
    return pressure, velocity


def on_device(
    guess_pressure, guess_velocity, initial_pressure, initial_velocity, stiffness, inv_mass
):
    groups = lax.axis_size("tm")
    group = lax.axis_index("tm")
    next_mass = from_behind(inv_mass[:1], "space", -1)

    both_p = jnp.stack([guess_pressure[0], initial_pressure])
    both_v = jnp.stack([guess_velocity[0], initial_velocity])
    first_p, first_v = propagate(both_p, both_v, stiffness, inv_mass, next_mass)
    relaxed_p, relaxed_v = first_p[0], first_v[0]
    own_end_p, own_end_v = first_p[1], first_v[1]

    shifted_p, shifted_v = from_behind((relaxed_p, relaxed_v), "tm", 1)
    late_p, late_v = propagate(shifted_p, shifted_v, stiffness, inv_mass, next_mass)
    first_group = group == 0
    end_p = jnp.where(first_group, own_end_p, late_p)
    end_v = jnp.where(first_group, own_end_v, late_v)
    resid_p = end_p - relaxed_p
    resid_v = end_v - relaxed_v

    if groups == 2:
        early_p = own_end_p - relaxed_p
        early_v = own_end_v - relaxed_v
        carried_p, carried_v = from_behind((early_p, early_v), "tm", 1)
        moved_p, moved_v = advance(carried_p, carried_v, stiffness, inv_mass, next_mass, DT_COARSE)
        error_p = resid_p + moved_p
        error_v = resid_v + moved_v
    else:
        error_p, error_v = resid_p, resid_v
        carried_p, carried_v = resid_p, resid_v
        for repeat in range(groups - 1):
            carried_p, carried_v = from_behind((carried_p, carried_v), "tm", 1)
            carried_p, carried_v = advance(
                carried_p, carried_v, stiffness, inv_mass, next_mass, DT_COARSE
            )
            error_p = error_p + carried_p
            error_v = error_v + carried_v
    corrected_p = relaxed_p + error_p
    corrected_v = relaxed_v + error_v
    return (corrected_p[None], corrected_v[None], resid_p[None], resid_v[None])


def solution(mesh):
    placed = (
        P("tm", "space", None, None),
        P("tm", None, "space", None, None),
        P("space", None, None),
        P(None, "space", None, None),
        P("space", None, None),
        P("space", None, None),
    )
    return jax.shard_map(
        on_device,
        mesh=mesh,
        in_specs=placed,
        out_specs=(
            P("tm", "space", None, None),
            P("tm", None, "space", None, None),
            P("tm", "space", None, None),
            P("tm", None, "space", None, None),
        ),
        check_vma=False,
    )
```

```python
import functools

import jax
import jax.numpy as jnp
from jax import lax
from jax.experimental import pallas as pl
from jax.experimental.pallas import tpu as pltpu
from jax.sharding import PartitionSpec as P

STEPS = 4


DT_COARSE = 0.4


def from_behind(x, axis, by):
    size = lax.axis_size(axis)
    pairs = [(i, i + by) for i in range(size) if 0 <= i + by < size]
    return lax.ppermute(x, axis, pairs)


def roll(x, shift, axis):
    return pltpu.roll(x, shift % x.shape[axis], axis)


def nsum(values, offset, axis):
    return values + roll(values, offset, axis)


def forces(pressure, lower):
    combined = pressure + lower
    force_x = 0.25 * (nsum(nsum(lower, 1, 1), 1, 0) - nsum(nsum(pressure, 1, 1), 1, 0))
    across_z = nsum(combined, 1, 1)
    force_y = 0.25 * (roll(across_z, 1, 0) - across_z)
    across_y = nsum(combined, 1, 0)
    force_z = 0.25 * (roll(across_y, 1, 1) - across_y)
    return force_x, force_y, force_z


def divergence(v, u):
    diff_x = nsum(nsum(u[0] - v[0], -1, 1), -1, 0)
    sum_y = nsum(v[1] + u[1], -1, 1)
    diff_y = roll(sum_y, -1, 0) - sum_y
    sum_z = nsum(v[2] + u[2], -1, 0)
    diff_z = roll(sum_z, -1, 1) - sum_z
    return 0.25 * (diff_x + diff_y + diff_z)


def upper_part(u):
    diff_x = nsum(nsum(u[0], -1, 1), -1, 0)
    sum_y = nsum(u[1], -1, 1)
    diff_y = roll(sum_y, -1, 0) - sum_y
    sum_z = nsum(u[2], -1, 0)
    diff_z = roll(sum_z, -1, 1) - sum_z
    return diff_x + diff_y + diff_z


def lower_part(v):
    diff_x = nsum(nsum(-v[0], -1, 1), -1, 0)
    sum_y = nsum(v[1], -1, 1)
    diff_y = roll(sum_y, -1, 0) - sum_y
    sum_z = nsum(v[2], -1, 0)
    diff_z = roll(sum_z, -1, 1) - sum_z
    return diff_x + diff_y + diff_z


def outgoing(pressure_first, velocity_first, mass_first, step_size):
    f = forces(pressure_first, jnp.zeros_like(pressure_first))
    hm = step_size * mass_first
    return upper_part([velocity_first[c] + hm * f[c] for c in range(3)])


def step_kernel(step_size, next_size, p_ref, v_ref, k_ref, m_ref, mn_ref, left_ref, right_ref,
                p_out, v_out, last_out, part_out):
    batch, n = p_ref.shape[0], p_ref.shape[1]
    for b in range(batch):
        pres = [p_ref[b, i] for i in range(n)]
        lower = [left_ref[b, 0]] + pres[:-1]
        vel = []
        for i in range(n):
            f = forces(pres[i], lower[i])
            hm = step_size * m_ref[i]
            vel.append([v_ref[b, c, i] + hm * f[c] for c in range(3)])
        for i in range(n):
            for c in range(3):
                v_out[b, c, i] = vel[i][c]
        new_p = []
        for i in range(n - 1):
            new_p.append(pres[i] - step_size * k_ref[i] * divergence(vel[i], vel[i + 1]))
        zero = jnp.zeros_like(pres[-1])
        hm_next = step_size * mn_ref[0]
        own_share = upper_part([hm_next * f for f in forces(zero, pres[-1])])
        edge = 0.25 * (lower_part(vel[-1]) + (right_ref[b, 0] + own_share))
        new_p.append(pres[-1] - step_size * k_ref[n - 1] * edge)
        for i in range(n):
            p_out[b, i] = new_p[i]
        last_out[b, 0] = new_p[-1]
        part_out[b, 0] = outgoing(new_p[0], vel[0], m_ref[0], next_size)


def prep_kernel(step_size, p_ref, v_ref, m_ref, last_out, part_out):
    batch, n = p_ref.shape[0], p_ref.shape[1]
    for b in range(batch):
        last_out[b, 0] = p_ref[b, n - 1]
        part_out[b, 0] = outgoing(p_ref[b, 0], [v_ref[b, c, 0] for c in range(3)], m_ref[0], step_size)


def prep(pressure, velocity, inv_mass, step_size):
    plane = jax.ShapeDtypeStruct((pressure.shape[0], 1) + pressure.shape[2:], pressure.dtype)
    return pl.pallas_call(
        functools.partial(prep_kernel, step_size), out_shape=(plane, plane)
    )(pressure, velocity, inv_mass)


def advance(state, stiffness, inv_mass, next_mass, step_size, next_size):
    pressure, velocity, last, share = state
    from_left = from_behind(last, "space", 1)
    from_right = from_behind(share, "space", -1)
    plane = jax.ShapeDtypeStruct(last.shape, last.dtype)
    outs = (
        jax.ShapeDtypeStruct(pressure.shape, pressure.dtype),
        jax.ShapeDtypeStruct(velocity.shape, velocity.dtype),
        plane,
        plane,
    )
    return pl.pallas_call(
        functools.partial(step_kernel, step_size, next_size), out_shape=outs
    )(pressure, velocity, stiffness, inv_mass, next_mass, from_left, from_right)


def propagate(pressure, velocity, stiffness, inv_mass, next_mass, after):
    fine_size = DT_COARSE / STEPS
    last, share = prep(pressure, velocity, inv_mass, fine_size)
    state = (pressure, velocity, last, share)
    for repeat in range(STEPS):
        following = fine_size if repeat + 1 < STEPS else after
        state = advance(state, stiffness, inv_mass, next_mass, fine_size, following)
    return state


def coarse(pressure, velocity, stiffness, inv_mass, next_mass):
    last, share = prep(pressure, velocity, inv_mass, DT_COARSE)
    state = advance((pressure, velocity, last, share), stiffness, inv_mass, next_mass, DT_COARSE, DT_COARSE)
    return state[0][0], state[1][0]


def on_device(
    guess_pressure, guess_velocity, initial_pressure, initial_velocity, stiffness, inv_mass
):
    groups = lax.axis_size("tm")
    group = lax.axis_index("tm")
    next_mass = from_behind(inv_mass[:1], "space", -1)

    both_p = jnp.stack([guess_pressure[0], initial_pressure])
    both_v = jnp.stack([guess_velocity[0], initial_velocity])
    first_p, first_v, _, _ = propagate(both_p, both_v, stiffness, inv_mass, next_mass, DT_COARSE)
    relaxed_p, relaxed_v = first_p[0], first_v[0]
    own_end_p, own_end_v = first_p[1], first_v[1]

    shifted_p, shifted_v = from_behind((relaxed_p, relaxed_v), "tm", 1)
    late_p, late_v, _, _ = propagate(
        shifted_p[None], shifted_v[None], stiffness, inv_mass, next_mass, DT_COARSE
    )
    first_group = group == 0
    end_p = jnp.where(first_group, own_end_p, late_p[0])
    end_v = jnp.where(first_group, own_end_v, late_v[0])
    resid_p = end_p - relaxed_p
    resid_v = end_v - relaxed_v

    if groups == 2:
        early_p = own_end_p - relaxed_p
        early_v = own_end_v - relaxed_v
        carried_p, carried_v = from_behind((early_p, early_v), "tm", 1)
        moved_p, moved_v = coarse(carried_p[None], carried_v[None], stiffness, inv_mass, next_mass)
        error_p = resid_p + moved_p
        error_v = resid_v + moved_v
    else:
        error_p, error_v = resid_p, resid_v
        carried_p, carried_v = resid_p, resid_v
        for repeat in range(groups - 1):
            carried_p, carried_v = from_behind((carried_p, carried_v), "tm", 1)
            carried_p, carried_v = coarse(
                carried_p[None], carried_v[None], stiffness, inv_mass, next_mass
            )
            error_p = error_p + carried_p
            error_v = error_v + carried_v
    corrected_p = relaxed_p + error_p
    corrected_v = relaxed_v + error_v
    return (corrected_p[None], corrected_v[None], resid_p[None], resid_v[None])


def solution(mesh):
    placed = (
        P("tm", "space", None, None),
        P("tm", None, "space", None, None),
        P("space", None, None),
        P(None, "space", None, None),
        P("space", None, None),
        P("space", None, None),
    )
    return jax.shard_map(
        on_device,
        mesh=mesh,
        in_specs=placed,
        out_specs=(
            P("tm", "space", None, None),
            P("tm", None, "space", None, None),
            P("tm", "space", None, None),
            P("tm", None, "space", None, None),
        ),
        check_vma=False,
    )
```

```python
import functools

import jax
import jax.numpy as jnp
from jax import lax
from jax.experimental import pallas as pl
from jax.experimental.pallas import tpu as pltpu
from jax.sharding import PartitionSpec as P

STEPS = 4


DT_COARSE = 0.4


def from_behind(x, axis, by):
    size = lax.axis_size(axis)
    pairs = [(i, i + by) for i in range(size) if 0 <= i + by < size]
    return lax.ppermute(x, axis, pairs)


def roll(x, shift, axis):
    return pltpu.roll(x, shift % x.shape[axis], axis)


def nsum(values, offset, axis):
    return values + roll(values, offset, axis)


def forces(pressure, lower):
    combined = pressure + lower
    force_x = 0.25 * (nsum(nsum(lower, 1, 1), 1, 0) - nsum(nsum(pressure, 1, 1), 1, 0))
    across_z = nsum(combined, 1, 1)
    force_y = 0.25 * (roll(across_z, 1, 0) - across_z)
    across_y = nsum(combined, 1, 0)
    force_z = 0.25 * (roll(across_y, 1, 1) - across_y)
    return force_x, force_y, force_z


def divergence(v, u):
    diff_x = nsum(nsum(u[0] - v[0], -1, 1), -1, 0)
    sum_y = nsum(v[1] + u[1], -1, 1)
    diff_y = roll(sum_y, -1, 0) - sum_y
    sum_z = nsum(v[2] + u[2], -1, 0)
    diff_z = roll(sum_z, -1, 1) - sum_z
    return 0.25 * (diff_x + diff_y + diff_z)


def upper_part(u):
    diff_x = nsum(nsum(u[0], -1, 1), -1, 0)
    sum_y = nsum(u[1], -1, 1)
    diff_y = roll(sum_y, -1, 0) - sum_y
    sum_z = nsum(u[2], -1, 0)
    diff_z = roll(sum_z, -1, 1) - sum_z
    return diff_x + diff_y + diff_z


def lower_part(v):
    diff_x = nsum(nsum(-v[0], -1, 1), -1, 0)
    sum_y = nsum(v[1], -1, 1)
    diff_y = roll(sum_y, -1, 0) - sum_y
    sum_z = nsum(v[2], -1, 0)
    diff_z = roll(sum_z, -1, 1) - sum_z
    return diff_x + diff_y + diff_z


def outgoing(pressure_first, velocity_first, mass_first, step_size):
    f = forces(pressure_first, jnp.zeros_like(pressure_first))
    hm = step_size * mass_first
    return upper_part([velocity_first[c] + hm * f[c] for c in range(3)])


def step_kernel(sizes, next_count, mass_index, emit_mass, s_ref, k_ref, m_ref, mn_ref, left_ref,
                right_ref, s_out, *outs):
    n = s_ref.shape[2]
    next_mass = mn_ref[mass_index, 0]
    for b, step_size in enumerate(sizes):
        pres = [s_ref[b, 0, i] for i in range(n)]
        lower = [left_ref[b, 0]] + pres[:-1]
        vel = []
        for i in range(n):
            f = forces(pres[i], lower[i])
            hm = step_size * m_ref[i]
            vel.append([s_ref[b, 1 + c, i] + hm * f[c] for c in range(3)])
        for i in range(n):
            for c in range(3):
                s_out[b, 1 + c, i] = vel[i][c]
        new_p = []
        for i in range(n - 1):
            new_p.append(pres[i] - step_size * k_ref[i] * divergence(vel[i], vel[i + 1]))
        zero = jnp.zeros_like(pres[-1])
        hm_next = step_size * next_mass
        own_share = upper_part([hm_next * f for f in forces(zero, pres[-1])])
        edge = 0.25 * (lower_part(vel[-1]) + (right_ref[b, 0] + own_share))
        new_p.append(pres[-1] - step_size * k_ref[n - 1] * edge)
        for i in range(n):
            s_out[b, 0, i] = new_p[i]
        if b < next_count:
            outs[0][b, 0] = new_p[-1]
            outs[1][b, 0] = outgoing(new_p[0], vel[0], m_ref[0], step_size)
    if emit_mass:
        outs[-1][0, 0] = next_mass


def plane_shape(count, like):
    return jax.ShapeDtypeStruct((count, 1) + like.shape[-2:], like.dtype)


def advance(state, last, share, stiffness, inv_mass, mass, sizes, next_count, mass_index=0):
    from_left = from_behind(last, "space", 1)
    from_right = from_behind(share, "space", -1)
    if mass is None:
        mass = from_right
    emit_mass = mass_index > 0
    outs = [jax.ShapeDtypeStruct((len(sizes),) + state.shape[1:], state.dtype)]
    if next_count:
        outs += [plane_shape(next_count, state), plane_shape(next_count, state)]
    if emit_mass:
        outs.append(plane_shape(1, state))
    return pl.pallas_call(
        functools.partial(step_kernel, tuple(sizes), next_count, mass_index, emit_mass),
        out_shape=tuple(outs),
    )(state, stiffness, inv_mass, mass, from_left, from_right)


def start_kernel(step_size, gp_ref, gv_ref, ip_ref, iv_ref, m_ref, s_out, last_out, part_out):
    n = ip_ref.shape[0]
    for i in range(n):
        s_out[0, 0, i] = gp_ref[0, i]
        s_out[1, 0, i] = ip_ref[i]
        for c in range(3):
            s_out[0, 1 + c, i] = gv_ref[0, c, i]
            s_out[1, 1 + c, i] = iv_ref[c, i]
    last_out[0, 0] = gp_ref[0, n - 1]
    last_out[1, 0] = ip_ref[n - 1]
    part_out[0, 0] = outgoing(gp_ref[0, 0], [gv_ref[0, c, 0] for c in range(3)], m_ref[0], step_size)
    part_out[1, 0] = outgoing(ip_ref[0], [iv_ref[c, 0] for c in range(3)], m_ref[0], step_size)
    part_out[2, 0] = m_ref[0]


def prep_kernel(sizes, s_ref, m_ref, last_out, part_out):
    n = s_ref.shape[2]
    for b, step_size in enumerate(sizes):
        last_out[b, 0] = s_ref[b, 0, n - 1]
        part_out[b, 0] = outgoing(
            s_ref[b, 0, 0], [s_ref[b, 1 + c, 0] for c in range(3)], m_ref[0], step_size
        )


def prep(state, inv_mass, sizes):
    return pl.pallas_call(
        functools.partial(prep_kernel, tuple(sizes)),
        out_shape=(plane_shape(len(sizes), state), plane_shape(len(sizes), state)),
    )(state, inv_mass)


def coarse(carried, stiffness, inv_mass, mass):
    last, share = prep(carried, inv_mass, (DT_COARSE,))
    (out,) = advance(carried, last, share, stiffness, inv_mass, mass, (DT_COARSE,), 0)
    return out[0]


def on_device(
    guess_pressure, guess_velocity, initial_pressure, initial_velocity, stiffness, inv_mass
):
    fine_size = DT_COARSE / STEPS
    groups = lax.axis_size("tm")
    group = lax.axis_index("tm")
    n = stiffness.shape[0]

    state_shape = jax.ShapeDtypeStruct((2, 4) + stiffness.shape, stiffness.dtype)
    state, last, share = pl.pallas_call(
        functools.partial(start_kernel, fine_size),
        out_shape=(state_shape, plane_shape(2, stiffness), plane_shape(3, stiffness)),
    )(guess_pressure, guess_velocity, initial_pressure, initial_velocity, inv_mass)
    state, last, share, mass = advance(
        state, last, share, stiffness, inv_mass, None, (fine_size, fine_size), 2, mass_index=2
    )
    for repeat in range(1, STEPS):
        count = 2 if repeat + 1 < STEPS else 0
        outs = advance(state, last, share, stiffness, inv_mass, mass, (fine_size, fine_size), count)
        state = outs[0]
        if count:
            last, share = outs[1], outs[2]
    relaxed, own_end = state[0], state[1]
    early = own_end - relaxed

    got = from_behind(jnp.stack([relaxed, early]), "tm", 1)
    last, share = prep(got, inv_mass, (fine_size, DT_COARSE))
    both, last, share = advance(got, last, share, stiffness, inv_mass, mass, (fine_size, DT_COARSE), 1)
    late = both
    for repeat in range(1, STEPS):
        count = 1 if repeat + 1 < STEPS else 0
        outs = advance(late, last, share, stiffness, inv_mass, mass, (fine_size,), count)
        late = outs[0]
        if count:
            last, share = outs[1], outs[2]

    end = jnp.where(group == 0, own_end, late[0])
    resid = end - relaxed
    if groups == 2:
        error = resid + both[1]
    else:
        error, carried = resid, resid
        for repeat in range(groups - 1):
            carried = from_behind(carried, "tm", 1)
            carried = coarse(carried[None], stiffness, inv_mass, mass)
            error = error + carried
    corrected = relaxed + error
    return (corrected[0][None], corrected[1:][None], resid[0][None], resid[1:][None])


def solution(mesh):
    placed = (
        P("tm", "space", None, None),
        P("tm", None, "space", None, None),
        P("space", None, None),
        P(None, "space", None, None),
        P("space", None, None),
        P("space", None, None),
    )
    return jax.shard_map(
        on_device,
        mesh=mesh,
        in_specs=placed,
        out_specs=(
            P("tm", "space", None, None),
            P("tm", None, "space", None, None),
            P("tm", "space", None, None),
            P("tm", None, "space", None, None),
        ),
        check_vma=False,
    )
```

```python
import functools

import jax
import jax.numpy as jnp
from jax import lax
from jax.experimental import pallas as pl
from jax.experimental.pallas import tpu as pltpu
from jax.sharding import PartitionSpec as P

STEPS = 4


DT_COARSE = 0.4


def from_behind(x, axis, by):
    size = lax.axis_size(axis)
    pairs = [(i, i + by) for i in range(size) if 0 <= i + by < size]
    return lax.ppermute(x, axis, pairs)


def roll(x, shift, axis):
    return pltpu.roll(x, shift % x.shape[axis], axis)


def nsum(values, offset, axis):
    return values + roll(values, offset, axis)


def forces(pressure, lower):
    combined = pressure + lower
    force_x = 0.25 * (nsum(nsum(lower, 1, 1), 1, 0) - nsum(nsum(pressure, 1, 1), 1, 0))
    across_z = nsum(combined, 1, 1)
    force_y = 0.25 * (roll(across_z, 1, 0) - across_z)
    across_y = nsum(combined, 1, 0)
    force_z = 0.25 * (roll(across_y, 1, 1) - across_y)
    return force_x, force_y, force_z


def divergence(v, u):
    diff_x = nsum(nsum(u[0] - v[0], -1, 1), -1, 0)
    sum_y = nsum(v[1] + u[1], -1, 1)
    diff_y = roll(sum_y, -1, 0) - sum_y
    sum_z = nsum(v[2] + u[2], -1, 0)
    diff_z = roll(sum_z, -1, 1) - sum_z
    return 0.25 * (diff_x + diff_y + diff_z)


def upper_part(u):
    diff_x = nsum(nsum(u[0], -1, 1), -1, 0)
    sum_y = nsum(u[1], -1, 1)
    diff_y = roll(sum_y, -1, 0) - sum_y
    sum_z = nsum(u[2], -1, 0)
    diff_z = roll(sum_z, -1, 1) - sum_z
    return diff_x + diff_y + diff_z


def lower_part(v):
    diff_x = nsum(nsum(-v[0], -1, 1), -1, 0)
    sum_y = nsum(v[1], -1, 1)
    diff_y = roll(sum_y, -1, 0) - sum_y
    sum_z = nsum(v[2], -1, 0)
    diff_z = roll(sum_z, -1, 1) - sum_z
    return diff_x + diff_y + diff_z


def outgoing(pressure_first, velocity_first, mass_first, step_size):
    f = forces(pressure_first, jnp.zeros_like(pressure_first))
    hm = step_size * mass_first
    return upper_part([velocity_first[c] + hm * f[c] for c in range(3)])


def messages(pres, vel, k_ref, m_ref, step_size):
    n = len(pres)
    last_node = [vel[n - 1][c] + step_size * m_ref[n - 1] * f
                 for c, f in enumerate(forces(pres[n - 1], pres[n - 2]))]
    behind = pres[n - 1] - step_size * k_ref[n - 1] * (0.25 * lower_part(last_node))
    f0 = forces(pres[0], jnp.zeros_like(pres[0]))
    partial = [vel[0][c] + step_size * m_ref[0] * f0[c] for c in range(3)]
    second = [vel[1][c] + step_size * m_ref[1] * f for c, f in enumerate(forces(pres[1], pres[0]))]
    ahead = pres[0] - step_size * k_ref[0] * (0.25 * (lower_part(partial) + upper_part(second)))
    return (pres[n - 1], behind), (upper_part(partial), ahead)


def plane_list(ref, b):
    n = ref.shape[2]
    return [ref[b, 0, i] for i in range(n)], [[ref[b, 1 + c, i] for c in range(3)] for i in range(n)]


def write_messages(b, msgs, right_out, left_out):
    (p_last, behind), (share, ahead) = msgs
    right_out[2 * b] = p_last
    right_out[2 * b + 1] = behind
    left_out[2 * b] = share
    left_out[2 * b + 1] = ahead


def pair_kernel(sizes, counts, next_count, first, s_ref, k_ref, m_ref, c_ref, fl_ref, fr_ref,
                s_out, *outs):
    n = s_ref.shape[2]
    width = 2 * len(sizes)
    if first:
        next_mass, next_stiff, prev_stiff = fr_ref[width], fr_ref[width + 1], fl_ref[width]
    else:
        next_mass, next_stiff, prev_stiff = c_ref[0], c_ref[1], c_ref[2]
    zero = jnp.zeros_like(next_mass)
    for b, (h, count) in enumerate(zip(sizes, counts)):
        pres, vel = plane_list(s_ref, b)
        lower = [fl_ref[2 * b]] + pres[:-1]
        vel1 = [[vel[i][c] + h * m_ref[i] * f for c, f in enumerate(forces(pres[i], lower[i]))]
                for i in range(n)]
        pres1 = [pres[i] - h * k_ref[i] * divergence(vel1[i], vel1[i + 1]) for i in range(n - 1)]
        below = [h * next_mass * f for f in forces(zero, pres[n - 1])]
        upper1 = fr_ref[2 * b] + upper_part(below)
        pres1.append(pres[n - 1] - h * k_ref[n - 1] * (0.25 * (lower_part(vel1[n - 1]) + upper1)))
        if count == 2:
            prev1 = fl_ref[2 * b + 1] - h * prev_stiff * (0.25 * upper_part(vel1[0]))
            next1 = fr_ref[2 * b + 1] - h * next_stiff * (0.25 * lower_part(below))
            lower = [prev1] + pres1[:-1]
            vel2 = [[vel1[i][c] + h * m_ref[i] * f for c, f in enumerate(forces(pres1[i], lower[i]))]
                    for i in range(n)]
            pres2 = [pres1[i] - h * k_ref[i] * divergence(vel2[i], vel2[i + 1]) for i in range(n - 1)]
            upper2 = upper1 + upper_part([h * next_mass * f for f in forces(next1, pres1[n - 1])])
            pres2.append(pres1[n - 1] - h * k_ref[n - 1] * (0.25 * (lower_part(vel2[n - 1]) + upper2)))
            pres1, vel1 = pres2, vel2
        for i in range(n):
            s_out[b, 0, i] = pres1[i]
            for c in range(3):
                s_out[b, 1 + c, i] = vel1[i][c]
        if b < next_count:
            write_messages(b, messages(pres1, vel1, k_ref, m_ref, h), outs[0], outs[1])
    if first:
        outs[-1][0] = next_mass
        outs[-1][1] = next_stiff
        outs[-1][2] = prev_stiff


def planes(count, like):
    return jax.ShapeDtypeStruct((count,) + like.shape[-2:], like.dtype)


def advance(state, to_right, to_left, stiffness, inv_mass, consts, sizes, counts, next_count):
    from_left = from_behind(to_right, "space", 1)
    from_right = from_behind(to_left, "space", -1)
    first = consts is None
    if first:
        consts = from_left
    outs = [jax.ShapeDtypeStruct((len(sizes),) + state.shape[1:], state.dtype)]
    if next_count:
        outs += [planes(2 * next_count, state), planes(2 * next_count, state)]
    if first:
        outs.append(planes(3, state))
    return pl.pallas_call(
        functools.partial(pair_kernel, tuple(sizes), tuple(counts), next_count, first),
        out_shape=tuple(outs),
    )(state, stiffness, inv_mass, consts, from_left, from_right)


def start_kernel(step_size, gp_ref, gv_ref, ip_ref, iv_ref, k_ref, m_ref, s_out, right_out, left_out):
    n = ip_ref.shape[0]
    sources = (
        ([gp_ref[0, i] for i in range(n)], [[gv_ref[0, c, i] for c in range(3)] for i in range(n)]),
        ([ip_ref[i] for i in range(n)], [[iv_ref[c, i] for c in range(3)] for i in range(n)]),
    )
    for b, (pres, vel) in enumerate(sources):
        for i in range(n):
            s_out[b, 0, i] = pres[i]
            for c in range(3):
                s_out[b, 1 + c, i] = vel[i][c]
        write_messages(b, messages(pres, vel, k_ref, m_ref, step_size), right_out, left_out)
    right_out[4] = k_ref[n - 1]
    left_out[4] = m_ref[0]
    left_out[5] = k_ref[0]


def late_kernel(sizes, got_ref, own_ref, k_ref, m_ref, s_out, right_out, left_out):
    n = got_ref.shape[1]
    for i in range(n):
        for c in range(4):
            s_out[0, c, i] = got_ref[c, i]
            s_out[1, c, i] = own_ref[1, c, i] - got_ref[c, i]
    for b, h in enumerate(sizes):
        pres, vel = plane_list(s_out, b)
        write_messages(b, messages(pres, vel, k_ref, m_ref, h), right_out, left_out)


def chain_kernel(step_size, s_ref, k_ref, m_ref, right_out, left_out):
    pres, vel = plane_list(s_ref, 0)
    write_messages(0, messages(pres, vel, k_ref, m_ref, step_size), right_out, left_out)


def coarse(carried, stiffness, inv_mass, consts):
    to_right, to_left = pl.pallas_call(
        functools.partial(chain_kernel, DT_COARSE),
        out_shape=(planes(2, carried), planes(2, carried)),
    )(carried, stiffness, inv_mass)
    (out,) = advance(carried, to_right, to_left, stiffness, inv_mass, consts, (DT_COARSE,), (1,), 0)
    return out[0]


def on_device(
    guess_pressure, guess_velocity, initial_pressure, initial_velocity, stiffness, inv_mass
):
    fine_size = DT_COARSE / STEPS
    groups = lax.axis_size("tm")
    group = lax.axis_index("tm")
    assert stiffness.shape[0] >= 2 and STEPS % 2 == 0

    state_shape = jax.ShapeDtypeStruct((2, 4) + stiffness.shape, stiffness.dtype)
    state, to_right, to_left = pl.pallas_call(
        functools.partial(start_kernel, fine_size),
        out_shape=(state_shape, planes(5, stiffness), planes(6, stiffness)),
    )(guess_pressure, guess_velocity, initial_pressure, initial_velocity, stiffness, inv_mass)
    rounds = STEPS // 2
    fine2 = (fine_size, fine_size)
    state, to_right, to_left, consts = advance(
        state, to_right, to_left, stiffness, inv_mass, None, fine2, (2, 2), 2 if rounds > 1 else 0
    )
    for repeat in range(1, rounds):
        count = 2 if repeat + 1 < rounds else 0
        outs = advance(state, to_right, to_left, stiffness, inv_mass, consts, fine2, (2, 2), count)
        state = outs[0]
        if count:
            to_right, to_left = outs[1], outs[2]
    relaxed, own_end = state[0], state[1]

    got = from_behind(relaxed, "tm", 1)
    late, to_right, to_left = pl.pallas_call(
        functools.partial(late_kernel, (fine_size, DT_COARSE)),
        out_shape=(state_shape, planes(4, stiffness), planes(4, stiffness)),
    )(got, state, stiffness, inv_mass)
    both = None
    for repeat in range(rounds):
        count = 1 if repeat + 1 < rounds else 0
        if repeat == 0:
            sizes, counts = (fine_size, DT_COARSE), (2, 1)
        else:
            sizes, counts = (fine_size,), (2,)
        outs = advance(late, to_right, to_left, stiffness, inv_mass, consts, sizes, counts, count)
        late = outs[0]
        if repeat == 0:
            both = late
        if count:
            to_right, to_left = outs[1], outs[2]

    end = jnp.where(group == 0, own_end, late[0])
    resid = end - relaxed
    if groups == 2:
        error = resid + jnp.where(group == 0, jnp.zeros_like(resid), both[1])
    else:
        error, carried = resid, resid
        for repeat in range(groups - 1):
            carried = from_behind(carried, "tm", 1)
            carried = coarse(carried[None], stiffness, inv_mass, consts)
            error = error + carried
    corrected = relaxed + error
    return (corrected[0][None], corrected[1:][None], resid[0][None], resid[1:][None])


def solution(mesh):
    placed = (
        P("tm", "space", None, None),
        P("tm", None, "space", None, None),
        P("space", None, None),
        P(None, "space", None, None),
        P("space", None, None),
        P("space", None, None),
    )
    return jax.shard_map(
        on_device,
        mesh=mesh,
        in_specs=placed,
        out_specs=(
            P("tm", "space", None, None),
            P("tm", None, "space", None, None),
            P("tm", "space", None, None),
            P("tm", None, "space", None, None),
        ),
        check_vma=False,
    )
```

```python
import functools

import jax
import jax.numpy as jnp
from jax import lax
from jax.experimental import pallas as pl
from jax.experimental.pallas import tpu as pltpu
from jax.sharding import PartitionSpec as P

STEPS = 4


DT_COARSE = 0.4


def from_behind(x, axis, by):
    size = lax.axis_size(axis)
    pairs = [(i, i + by) for i in range(size) if 0 <= i + by < size]
    return lax.ppermute(x, axis, pairs)


def roll(x, shift, axis):
    return pltpu.roll(x, shift % x.shape[axis], axis)


def nsum(values, offset, axis):
    return values + roll(values, offset, axis)


def forces(pressure, lower):
    combined = pressure + lower
    force_x = 0.25 * (nsum(nsum(lower, 1, 1), 1, 0) - nsum(nsum(pressure, 1, 1), 1, 0))
    across_z = nsum(combined, 1, 1)
    force_y = 0.25 * (roll(across_z, 1, 0) - across_z)
    across_y = nsum(combined, 1, 0)
    force_z = 0.25 * (roll(across_y, 1, 1) - across_y)
    return force_x, force_y, force_z


def divergence(v, u):
    diff_x = nsum(nsum(u[0] - v[0], -1, 1), -1, 0)
    sum_y = nsum(v[1] + u[1], -1, 1)
    diff_y = roll(sum_y, -1, 0) - sum_y
    sum_z = nsum(v[2] + u[2], -1, 0)
    diff_z = roll(sum_z, -1, 1) - sum_z
    return 0.25 * (diff_x + diff_y + diff_z)


def upper_part(u):
    diff_x = nsum(nsum(u[0], -1, 1), -1, 0)
    sum_y = nsum(u[1], -1, 1)
    diff_y = roll(sum_y, -1, 0) - sum_y
    sum_z = nsum(u[2], -1, 0)
    diff_z = roll(sum_z, -1, 1) - sum_z
    return diff_x + diff_y + diff_z


def lower_part(v):
    diff_x = nsum(nsum(-v[0], -1, 1), -1, 0)
    sum_y = nsum(v[1], -1, 1)
    diff_y = roll(sum_y, -1, 0) - sum_y
    sum_z = nsum(v[2], -1, 0)
    diff_z = roll(sum_z, -1, 1) - sum_z
    return diff_x + diff_y + diff_z


def outgoing(pressure_first, velocity_first, mass_first, step_size):
    f = forces(pressure_first, jnp.zeros_like(pressure_first))
    hm = step_size * mass_first
    return upper_part([velocity_first[c] + hm * f[c] for c in range(3)])


def messages(pres, vel, k_ref, m_ref, step_size):
    n = len(pres)
    last_node = [vel[n - 1][c] + step_size * m_ref[n - 1] * f
                 for c, f in enumerate(forces(pres[n - 1], pres[n - 2]))]
    behind = pres[n - 1] - step_size * k_ref[n - 1] * (0.25 * lower_part(last_node))
    f0 = forces(pres[0], jnp.zeros_like(pres[0]))
    partial = [vel[0][c] + step_size * m_ref[0] * f0[c] for c in range(3)]
    second = [vel[1][c] + step_size * m_ref[1] * f for c, f in enumerate(forces(pres[1], pres[0]))]
    ahead = pres[0] - step_size * k_ref[0] * (0.25 * (lower_part(partial) + upper_part(second)))
    return (pres[n - 1], behind), (upper_part(partial), ahead)


def plane_list(ref, b):
    n = ref.shape[2]
    return [ref[b, 0, i] for i in range(n)], [[ref[b, 1 + c, i] for c in range(3)] for i in range(n)]


def write_messages(b, msgs, right_out, left_out):
    (p_last, behind), (share, ahead) = msgs
    right_out[2 * b] = p_last
    right_out[2 * b + 1] = behind
    left_out[2 * b] = share
    left_out[2 * b + 1] = ahead


def pair_kernel(sizes, counts, next_count, first, split, s_ref, k_ref, m_ref, c_ref, fl_ref, fr_ref,
                s_out, *outs):
    n = s_ref.shape[2]
    width = 2 * len(sizes)
    if first:
        next_mass, next_stiff, prev_stiff = fr_ref[width], fr_ref[width + 1], fl_ref[width]
    else:
        next_mass, next_stiff, prev_stiff = c_ref[0], c_ref[1], c_ref[2]
    zero = jnp.zeros_like(next_mass)
    for b, (h, count) in enumerate(zip(sizes, counts)):
        pres, vel = plane_list(s_ref, b)
        lower = [fl_ref[2 * b]] + pres[:-1]
        vel1 = [[vel[i][c] + h * m_ref[i] * f for c, f in enumerate(forces(pres[i], lower[i]))]
                for i in range(n)]
        pres1 = [pres[i] - h * k_ref[i] * divergence(vel1[i], vel1[i + 1]) for i in range(n - 1)]
        below = [h * next_mass * f for f in forces(zero, pres[n - 1])]
        upper1 = fr_ref[2 * b] + upper_part(below)
        pres1.append(pres[n - 1] - h * k_ref[n - 1] * (0.25 * (lower_part(vel1[n - 1]) + upper1)))
        if count == 2:
            prev1 = fl_ref[2 * b + 1] - h * prev_stiff * (0.25 * upper_part(vel1[0]))
            next1 = fr_ref[2 * b + 1] - h * next_stiff * (0.25 * lower_part(below))
            lower = [prev1] + pres1[:-1]
            vel2 = [[vel1[i][c] + h * m_ref[i] * f for c, f in enumerate(forces(pres1[i], lower[i]))]
                    for i in range(n)]
            pres2 = [pres1[i] - h * k_ref[i] * divergence(vel2[i], vel2[i + 1]) for i in range(n - 1)]
            upper2 = upper1 + upper_part([h * next_mass * f for f in forces(next1, pres1[n - 1])])
            pres2.append(pres1[n - 1] - h * k_ref[n - 1] * (0.25 * (lower_part(vel2[n - 1]) + upper2)))
            pres1, vel1 = pres2, vel2
        for i in range(n):
            s_out[b, 0, i] = pres1[i]
            for c in range(3):
                s_out[b, 1 + c, i] = vel1[i][c]
            if split and b == 0:
                outs[-1][0, i] = pres1[i]
                for c in range(3):
                    outs[-1][1 + c, i] = vel1[i][c]
        if b < next_count:
            write_messages(b, messages(pres1, vel1, k_ref, m_ref, h), outs[0], outs[1])
    if first:
        outs[2 if next_count else 0][0] = next_mass
        outs[2 if next_count else 0][1] = next_stiff
        outs[2 if next_count else 0][2] = prev_stiff


def planes(count, like):
    return jax.ShapeDtypeStruct((count,) + like.shape[-2:], like.dtype)


def advance(state, to_right, to_left, stiffness, inv_mass, consts, sizes, counts, next_count, split=False):
    from_left = from_behind(to_right, "space", 1)
    from_right = from_behind(to_left, "space", -1)
    first = consts is None
    if first:
        consts = from_left
    outs = [jax.ShapeDtypeStruct((len(sizes),) + state.shape[1:], state.dtype)]
    if next_count:
        outs += [planes(2 * next_count, state), planes(2 * next_count, state)]
    if first:
        outs.append(planes(3, state))
    if split:
        outs.append(jax.ShapeDtypeStruct(state.shape[1:], state.dtype))
    return pl.pallas_call(
        functools.partial(pair_kernel, tuple(sizes), tuple(counts), next_count, first, split),
        out_shape=tuple(outs),
    )(state, stiffness, inv_mass, consts, from_left, from_right)


def start_kernel(step_size, gp_ref, gv_ref, ip_ref, iv_ref, k_ref, m_ref, s_out, right_out, left_out):
    n = ip_ref.shape[0]
    sources = (
        ([gp_ref[0, i] for i in range(n)], [[gv_ref[0, c, i] for c in range(3)] for i in range(n)]),
        ([ip_ref[i] for i in range(n)], [[iv_ref[c, i] for c in range(3)] for i in range(n)]),
    )
    for b, (pres, vel) in enumerate(sources):
        for i in range(n):
            s_out[b, 0, i] = pres[i]
            for c in range(3):
                s_out[b, 1 + c, i] = vel[i][c]
        write_messages(b, messages(pres, vel, k_ref, m_ref, step_size), right_out, left_out)
    right_out[4] = k_ref[n - 1]
    left_out[4] = m_ref[0]
    left_out[5] = k_ref[0]


def late_kernel(sizes, got_ref, own_ref, k_ref, m_ref, s_out, right_out, left_out):
    n = got_ref.shape[1]
    for i in range(n):
        for c in range(4):
            s_out[0, c, i] = got_ref[c, i]
            s_out[1, c, i] = own_ref[1, c, i] - got_ref[c, i]
    for b, h in enumerate(sizes):
        pres, vel = plane_list(s_out, b)
        write_messages(b, messages(pres, vel, k_ref, m_ref, h), right_out, left_out)


def chain_kernel(step_size, s_ref, k_ref, m_ref, right_out, left_out):
    pres, vel = plane_list(s_ref, 0)
    write_messages(0, messages(pres, vel, k_ref, m_ref, step_size), right_out, left_out)


def coarse(carried, stiffness, inv_mass, consts):
    to_right, to_left = pl.pallas_call(
        functools.partial(chain_kernel, DT_COARSE),
        out_shape=(planes(2, carried), planes(2, carried)),
    )(carried, stiffness, inv_mass)
    (out,) = advance(carried, to_right, to_left, stiffness, inv_mass, consts, (DT_COARSE,), (1,), 0)
    return out[0]


def finish_kernel(g_ref, s_ref, late_ref, both_ref, cp_out, cv_out, rp_out, rv_out):
    n = s_ref.shape[2]

    def write(end_ref, moved):
        for i in range(n):
            for c in range(4):
                relaxed = s_ref[0, c, i]
                resid = end_ref[c, i] - relaxed
                error = resid if moved is None else resid + moved[c, i]
                if c == 0:
                    rp_out[0, i] = resid
                    cp_out[0, i] = relaxed + error
                else:
                    rv_out[0, c - 1, i] = resid
                    cv_out[0, c - 1, i] = relaxed + error

    @pl.when(g_ref[0] == 0)
    def _():
        write(s_ref.at[1], None)

    @pl.when(g_ref[0] != 0)
    def _():
        write(late_ref.at[0], both_ref.at[1])


def on_device(
    guess_pressure, guess_velocity, initial_pressure, initial_velocity, stiffness, inv_mass
):
    fine_size = DT_COARSE / STEPS
    groups = lax.axis_size("tm")
    group = lax.axis_index("tm")
    assert stiffness.shape[0] >= 2 and STEPS % 2 == 0

    state_shape = jax.ShapeDtypeStruct((2, 4) + stiffness.shape, stiffness.dtype)
    state, to_right, to_left = pl.pallas_call(
        functools.partial(start_kernel, fine_size),
        out_shape=(state_shape, planes(5, stiffness), planes(6, stiffness)),
    )(guess_pressure, guess_velocity, initial_pressure, initial_velocity, stiffness, inv_mass)
    rounds = STEPS // 2
    fine2 = (fine_size, fine_size)
    state, to_right, to_left, consts = advance(
        state, to_right, to_left, stiffness, inv_mass, None, fine2, (2, 2), 2 if rounds > 1 else 0
    )
    for repeat in range(1, rounds):
        count = 2 if repeat + 1 < rounds else 0
        outs = advance(
            state, to_right, to_left, stiffness, inv_mass, consts, fine2, (2, 2), count,
            split=repeat + 1 == rounds,
        )
        state = outs[0]
        if count:
            to_right, to_left = outs[1], outs[2]
    relaxed = outs[-1]

    got = from_behind(relaxed, "tm", 1)
    late, to_right, to_left = pl.pallas_call(
        functools.partial(late_kernel, (fine_size, DT_COARSE)),
        out_shape=(state_shape, planes(4, stiffness), planes(4, stiffness)),
    )(got, state, stiffness, inv_mass)
    both = None
    for repeat in range(rounds):
        count = 1 if repeat + 1 < rounds else 0
        if repeat == 0:
            sizes, counts = (fine_size, DT_COARSE), (2, 1)
        else:
            sizes, counts = (fine_size,), (2,)
        outs = advance(late, to_right, to_left, stiffness, inv_mass, consts, sizes, counts, count)
        late = outs[0]
        if repeat == 0:
            both = late
        if count:
            to_right, to_left = outs[1], outs[2]

    if groups == 2:
        flat = jax.ShapeDtypeStruct((1,) + stiffness.shape, stiffness.dtype)
        vflat = jax.ShapeDtypeStruct((1, 3) + stiffness.shape, stiffness.dtype)
        vmem = pl.BlockSpec(memory_space=pltpu.VMEM)
        return pl.pallas_call(
            finish_kernel,
            out_shape=(flat, vflat, flat, vflat),
            in_specs=[pl.BlockSpec(memory_space=pltpu.SMEM), vmem, vmem, vmem],
        )(jnp.reshape(group, (1,)).astype(jnp.int32), state, late, both)
    end = jnp.where(group == 0, state[1], late[0])
    resid = end - relaxed
    error, carried = resid, resid
    for repeat in range(groups - 1):
        carried = from_behind(carried, "tm", 1)
        carried = coarse(carried[None], stiffness, inv_mass, consts)
        error = error + carried
    corrected = relaxed + error
    return (corrected[0][None], corrected[1:][None], resid[0][None], resid[1:][None])


def solution(mesh):
    placed = (
        P("tm", "space", None, None),
        P("tm", None, "space", None, None),
        P("space", None, None),
        P(None, "space", None, None),
        P("space", None, None),
        P("space", None, None),
    )
    return jax.shard_map(
        on_device,
        mesh=mesh,
        in_specs=placed,
        out_specs=(
            P("tm", "space", None, None),
            P("tm", None, "space", None, None),
            P("tm", "space", None, None),
            P("tm", None, "space", None, None),
        ),
        check_vma=False,
    )
```

```python
import functools

import jax
import jax.numpy as jnp
from jax import lax
from jax.experimental import pallas as pl
from jax.experimental.pallas import tpu as pltpu
from jax.sharding import PartitionSpec as P

STEPS = 4


DT_COARSE = 0.4


def from_behind(x, axis, by):
    size = lax.axis_size(axis)
    pairs = [(i, i + by) for i in range(size) if 0 <= i + by < size]
    return lax.ppermute(x, axis, pairs)


def roll(x, shift, axis):
    return pltpu.roll(x, shift % x.shape[axis], axis)


def nsum(values, offset, axis):
    return values + roll(values, offset, axis)


def forces(pressure, lower):
    combined = pressure + lower
    force_x = 0.25 * (nsum(nsum(lower, 1, 1), 1, 0) - nsum(nsum(pressure, 1, 1), 1, 0))
    across_z = nsum(combined, 1, 1)
    force_y = 0.25 * (roll(across_z, 1, 0) - across_z)
    across_y = nsum(combined, 1, 0)
    force_z = 0.25 * (roll(across_y, 1, 1) - across_y)
    return force_x, force_y, force_z


def divergence(v, u):
    diff_x = nsum(nsum(u[0] - v[0], -1, 1), -1, 0)
    sum_y = nsum(v[1] + u[1], -1, 1)
    diff_y = roll(sum_y, -1, 0) - sum_y
    sum_z = nsum(v[2] + u[2], -1, 0)
    diff_z = roll(sum_z, -1, 1) - sum_z
    return 0.25 * (diff_x + diff_y + diff_z)


def upper_part(u):
    diff_x = nsum(nsum(u[0], -1, 1), -1, 0)
    sum_y = nsum(u[1], -1, 1)
    diff_y = roll(sum_y, -1, 0) - sum_y
    sum_z = nsum(u[2], -1, 0)
    diff_z = roll(sum_z, -1, 1) - sum_z
    return diff_x + diff_y + diff_z


def lower_part(v):
    diff_x = nsum(nsum(-v[0], -1, 1), -1, 0)
    sum_y = nsum(v[1], -1, 1)
    diff_y = roll(sum_y, -1, 0) - sum_y
    sum_z = nsum(v[2], -1, 0)
    diff_z = roll(sum_z, -1, 1) - sum_z
    return diff_x + diff_y + diff_z


def outgoing(pressure_first, velocity_first, mass_first, step_size):
    f = forces(pressure_first, jnp.zeros_like(pressure_first))
    hm = step_size * mass_first
    return upper_part([velocity_first[c] + hm * f[c] for c in range(3)])


def messages(pres, vel, k_ref, m_ref, step_size):
    n = len(pres)
    last_node = [vel[n - 1][c] + step_size * m_ref[n - 1] * f
                 for c, f in enumerate(forces(pres[n - 1], pres[n - 2]))]
    behind = pres[n - 1] - step_size * k_ref[n - 1] * (0.25 * lower_part(last_node))
    f0 = forces(pres[0], jnp.zeros_like(pres[0]))
    partial = [vel[0][c] + step_size * m_ref[0] * f0[c] for c in range(3)]
    second = [vel[1][c] + step_size * m_ref[1] * f for c, f in enumerate(forces(pres[1], pres[0]))]
    ahead = pres[0] - step_size * k_ref[0] * (0.25 * (lower_part(partial) + upper_part(second)))
    return (pres[n - 1], behind), (upper_part(partial), ahead)


def read_slot(source, refs, n):
    kind = source[0]
    if kind == "packed":
        ref, b = refs[source[1]], source[2]
        get = lambda c, i: ref[b, c, i]
    elif kind == "flat":
        ref = refs[source[1]]
        get = lambda c, i: ref[c, i]
    elif kind == "diff":
        ref, b, other = refs[source[1]], source[2], refs[source[3]]
        get = lambda c, i: ref[b, c, i] - other[c, i]
    else:
        pref, vref, lead = refs[source[1]], refs[source[2]], source[3]
        if lead:
            get = lambda c, i: pref[0, i] if c == 0 else vref[0, c - 1, i]
        else:
            get = lambda c, i: pref[i] if c == 0 else vref[c - 1, i]
    return [get(0, i) for i in range(n)], [[get(1 + c, i) for c in range(3)] for i in range(n)]


def write_messages(b, msgs, right_out, left_out):
    (p_last, behind), (share, ahead) = msgs
    right_out[2 * b] = p_last
    right_out[2 * b + 1] = behind
    left_out[2 * b] = share
    left_out[2 * b + 1] = ahead


def write_outputs(g_ref, st_ref, moved_ref, late, n, outs):
    cp_out, cv_out, rp_out, rv_out = outs

    def write(end_of, moved_of):
        for i in range(n):
            for c in range(4):
                relaxed = st_ref[0, c, i]
                resid = end_of(c, i) - relaxed
                error = resid if moved_of is None else resid + moved_of(c, i)
                if c == 0:
                    rp_out[0, i] = resid
                    cp_out[0, i] = relaxed + error
                else:
                    rv_out[0, c - 1, i] = resid
                    cv_out[0, c - 1, i] = relaxed + error

    @pl.when(g_ref[0] == 0)
    def _():
        write(lambda c, i: st_ref[1, c, i], None)

    @pl.when(g_ref[0] != 0)
    def _():
        write(lambda c, i: late[c][i], lambda c, i: moved_ref[1, c, i])


def pair_kernel(sizes, counts, sources, n_states, next_count, first, split, finish, *refs):
    states = refs[:n_states]
    k_ref, m_ref, c_ref, fl_ref, fr_ref = refs[n_states : n_states + 5]
    rest = refs[n_states + 5 :]
    if finish:
        g_ref, st_ref, moved_ref = rest[:3]
        outs = rest[3:]
    else:
        s_out = rest[0]
        outs = rest[1:]
    n = k_ref.shape[0]
    width = 2 * len(sizes)
    if first:
        next_mass, next_stiff, prev_stiff = fr_ref[width], fr_ref[width + 1], fl_ref[width]
    else:
        next_mass, next_stiff, prev_stiff = c_ref[0], c_ref[1], c_ref[2]
    zero = jnp.zeros_like(next_mass)
    for b, (h, count) in enumerate(zip(sizes, counts)):
        pres, vel = read_slot(sources[b], states, n)
        lower = [fl_ref[2 * b]] + pres[:-1]
        vel1 = [[vel[i][c] + h * m_ref[i] * f for c, f in enumerate(forces(pres[i], lower[i]))]
                for i in range(n)]
        pres1 = [pres[i] - h * k_ref[i] * divergence(vel1[i], vel1[i + 1]) for i in range(n - 1)]
        below = [h * next_mass * f for f in forces(zero, pres[n - 1])]
        upper1 = fr_ref[2 * b] + upper_part(below)
        pres1.append(pres[n - 1] - h * k_ref[n - 1] * (0.25 * (lower_part(vel1[n - 1]) + upper1)))
        if count == 2:
            prev1 = fl_ref[2 * b + 1] - h * prev_stiff * (0.25 * upper_part(vel1[0]))
            next1 = fr_ref[2 * b + 1] - h * next_stiff * (0.25 * lower_part(below))
            lower = [prev1] + pres1[:-1]
            vel2 = [[vel1[i][c] + h * m_ref[i] * f for c, f in enumerate(forces(pres1[i], lower[i]))]
                    for i in range(n)]
            pres2 = [pres1[i] - h * k_ref[i] * divergence(vel2[i], vel2[i + 1]) for i in range(n - 1)]
            upper2 = upper1 + upper_part([h * next_mass * f for f in forces(next1, pres1[n - 1])])
            pres2.append(pres1[n - 1] - h * k_ref[n - 1] * (0.25 * (lower_part(vel2[n - 1]) + upper2)))
            pres1, vel1 = pres2, vel2
        if finish:
            late = [pres1] + [[vel1[i][c] for i in range(n)] for c in range(3)]
            write_outputs(g_ref, st_ref, moved_ref, late, n, outs)
            continue
        for i in range(n):
            s_out[b, 0, i] = pres1[i]
            for c in range(3):
                s_out[b, 1 + c, i] = vel1[i][c]
            if split and b == 0:
                outs[-1][0, i] = pres1[i]
                for c in range(3):
                    outs[-1][1 + c, i] = vel1[i][c]
        if b < next_count:
            write_messages(b, messages(pres1, vel1, k_ref, m_ref, h), outs[0], outs[1])
    if first:
        outs[2 if next_count else 0][0] = next_mass
        outs[2 if next_count else 0][1] = next_stiff
        outs[2 if next_count else 0][2] = prev_stiff


def planes(count, like):
    return jax.ShapeDtypeStruct((count,) + like.shape[-2:], like.dtype)


def advance(states, sources, to_right, to_left, stiffness, inv_mass, consts, sizes, counts,
            next_count, split=False, finish=None):
    from_left = from_behind(to_right, "space", 1)
    from_right = from_behind(to_left, "space", -1)
    first = consts is None
    if first:
        consts = from_left
    n = stiffness.shape[0]
    args = list(states) + [stiffness, inv_mass, consts, from_left, from_right]
    vmem = pl.BlockSpec(memory_space=pltpu.VMEM)
    specs = [vmem] * len(args)
    if finish is not None:
        flat = jax.ShapeDtypeStruct((1,) + stiffness.shape, stiffness.dtype)
        vflat = jax.ShapeDtypeStruct((1, 3) + stiffness.shape, stiffness.dtype)
        outs = [flat, vflat, flat, vflat]
        args += list(finish)
        specs += [pl.BlockSpec(memory_space=pltpu.SMEM), vmem, vmem]
    else:
        outs = [jax.ShapeDtypeStruct((len(sizes), 4) + stiffness.shape, stiffness.dtype)]
        if next_count:
            outs += [planes(2 * next_count, stiffness), planes(2 * next_count, stiffness)]
        if first:
            outs.append(planes(3, stiffness))
        if split:
            outs.append(jax.ShapeDtypeStruct((4,) + stiffness.shape, stiffness.dtype))
    kernel = functools.partial(
        pair_kernel, tuple(sizes), tuple(counts), tuple(sources), len(states), next_count, first,
        split, finish is not None,
    )
    return pl.pallas_call(kernel, out_shape=tuple(outs), in_specs=specs)(*args)


def messages_kernel(sizes, sources, n_states, extras, *refs):
    states = refs[:n_states]
    k_ref, m_ref, right_out, left_out = refs[n_states:]
    n = k_ref.shape[0]
    for b, h in enumerate(sizes):
        pres, vel = read_slot(sources[b], states, n)
        write_messages(b, messages(pres, vel, k_ref, m_ref, h), right_out, left_out)
    if extras:
        width = 2 * len(sizes)
        right_out[width] = k_ref[n - 1]
        left_out[width] = m_ref[0]
        left_out[width + 1] = k_ref[0]


def first_messages(states, sources, stiffness, inv_mass, sizes, extras=False):
    width = 2 * len(sizes)
    kernel = functools.partial(messages_kernel, tuple(sizes), tuple(sources), len(states), extras)
    return pl.pallas_call(
        kernel,
        out_shape=(planes(width + (1 if extras else 0), stiffness), planes(width + (2 if extras else 0), stiffness)),
    )(*states, stiffness, inv_mass)


def coarse(carried, stiffness, inv_mass, consts):
    sources = (("flat", 0),)
    to_right, to_left = first_messages((carried,), sources, stiffness, inv_mass, (DT_COARSE,))
    (out,) = advance((carried,), sources, to_right, to_left, stiffness, inv_mass, consts,
                     (DT_COARSE,), (1,), 0)
    return out[0]


def on_device(
    guess_pressure, guess_velocity, initial_pressure, initial_velocity, stiffness, inv_mass
):
    fine_size = DT_COARSE / STEPS
    groups = lax.axis_size("tm")
    group = lax.axis_index("tm")
    assert stiffness.shape[0] >= 2 and STEPS % 2 == 0
    rounds = STEPS // 2
    fine2 = (fine_size, fine_size)

    inputs = (guess_pressure, guess_velocity, initial_pressure, initial_velocity)
    sources = (("input", 0, 1, True), ("input", 2, 3, False))
    to_right, to_left = first_messages(inputs, sources, stiffness, inv_mass, fine2, extras=True)
    state, to_right, to_left, consts = advance(
        inputs, sources, to_right, to_left, stiffness, inv_mass, None, fine2, (2, 2), 2,
    )
    packed = (("packed", 0, 0), ("packed", 0, 1))
    for repeat in range(1, rounds):
        count = 2 if repeat + 1 < rounds else 0
        outs = advance(
            (state,), packed, to_right, to_left, stiffness, inv_mass, consts, fine2, (2, 2), count,
            split=repeat + 1 == rounds,
        )
        state = outs[0]
        if count:
            to_right, to_left = outs[1], outs[2]
    relaxed = outs[-1]

    got = from_behind(relaxed, "tm", 1)
    late_states = (got, state)
    late_sources = (("flat", 0), ("diff", 1, 1, 0))
    to_right, to_left = first_messages(
        late_states, late_sources, stiffness, inv_mass, (fine_size, DT_COARSE)
    )
    flag = jnp.reshape(group, (1,)).astype(jnp.int32)
    both = None
    late = None
    for repeat in range(rounds):
        count = 1 if repeat + 1 < rounds else 0
        if repeat == 0:
            sizes, counts, states, srcs = (fine_size, DT_COARSE), (2, 1), late_states, late_sources
        else:
            sizes, counts, states, srcs = (fine_size,), (2,), (late,), (("packed", 0, 0),)
        finish = (flag, state, both) if (groups == 2 and repeat + 1 == rounds) else None
        outs = advance(states, srcs, to_right, to_left, stiffness, inv_mass, consts, sizes, counts,
                       count, finish=finish)
        if finish is not None:
            return outs
        late = outs[0]
        if repeat == 0:
            both = late
        if count:
            to_right, to_left = outs[1], outs[2]

    end = jnp.where(group == 0, state[1], late[0])
    resid = end - relaxed
    error, carried = resid, resid
    for repeat in range(groups - 1):
        carried = from_behind(carried, "tm", 1)
        carried = coarse(carried, stiffness, inv_mass, consts)
        error = error + carried
    corrected = relaxed + error
    return (corrected[0][None], corrected[1:][None], resid[0][None], resid[1:][None])


def solution(mesh):
    placed = (
        P("tm", "space", None, None),
        P("tm", None, "space", None, None),
        P("space", None, None),
        P(None, "space", None, None),
        P("space", None, None),
        P("space", None, None),
    )
    return jax.shard_map(
        on_device,
        mesh=mesh,
        in_specs=placed,
        out_specs=(
            P("tm", "space", None, None),
            P("tm", None, "space", None, None),
            P("tm", "space", None, None),
            P("tm", None, "space", None, None),
        ),
        check_vma=False,
    )
```

```python
import functools

import jax
import jax.numpy as jnp
from jax import lax
from jax.experimental import pallas as pl
from jax.experimental.pallas import tpu as pltpu
from jax.sharding import PartitionSpec as P

STEPS = 4


DT_COARSE = 0.4


def from_behind(x, axis, by):
    size = lax.axis_size(axis)
    pairs = [(i, i + by) for i in range(size) if 0 <= i + by < size]
    return lax.ppermute(x, axis, pairs)


def roll(x, shift, axis):
    return pltpu.roll(x, shift % x.shape[axis], axis)


def nsum(values, offset, axis):
    return values + roll(values, offset, axis)


def forces(pressure, lower):
    combined = pressure + lower
    force_x = 0.25 * (nsum(nsum(lower, 1, 1), 1, 0) - nsum(nsum(pressure, 1, 1), 1, 0))
    across_z = nsum(combined, 1, 1)
    force_y = 0.25 * (roll(across_z, 1, 0) - across_z)
    across_y = nsum(combined, 1, 0)
    force_z = 0.25 * (roll(across_y, 1, 1) - across_y)
    return force_x, force_y, force_z


def divergence(v, u):
    diff_x = nsum(nsum(u[0] - v[0], -1, 1), -1, 0)
    sum_y = nsum(v[1] + u[1], -1, 1)
    diff_y = roll(sum_y, -1, 0) - sum_y
    sum_z = nsum(v[2] + u[2], -1, 0)
    diff_z = roll(sum_z, -1, 1) - sum_z
    return 0.25 * (diff_x + diff_y + diff_z)


def upper_part(u):
    diff_x = nsum(nsum(u[0], -1, 1), -1, 0)
    sum_y = nsum(u[1], -1, 1)
    diff_y = roll(sum_y, -1, 0) - sum_y
    sum_z = nsum(u[2], -1, 0)
    diff_z = roll(sum_z, -1, 1) - sum_z
    return diff_x + diff_y + diff_z


def lower_part(v):
    diff_x = nsum(nsum(-v[0], -1, 1), -1, 0)
    sum_y = nsum(v[1], -1, 1)
    diff_y = roll(sum_y, -1, 0) - sum_y
    sum_z = nsum(v[2], -1, 0)
    diff_z = roll(sum_z, -1, 1) - sum_z
    return diff_x + diff_y + diff_z


def outgoing(pressure_first, velocity_first, mass_first, step_size):
    f = forces(pressure_first, jnp.zeros_like(pressure_first))
    hm = step_size * mass_first
    return upper_part([velocity_first[c] + hm * f[c] for c in range(3)])


def messages(pres, vel, k_ref, m_ref, step_size):
    n = len(pres)
    last_node = [vel[n - 1][c] + step_size * m_ref[n - 1] * f
                 for c, f in enumerate(forces(pres[n - 1], pres[n - 2]))]
    behind = pres[n - 1] - step_size * k_ref[n - 1] * (0.25 * lower_part(last_node))
    f0 = forces(pres[0], jnp.zeros_like(pres[0]))
    partial = [vel[0][c] + step_size * m_ref[0] * f0[c] for c in range(3)]
    second = [vel[1][c] + step_size * m_ref[1] * f for c, f in enumerate(forces(pres[1], pres[0]))]
    ahead = pres[0] - step_size * k_ref[0] * (0.25 * (lower_part(partial) + upper_part(second)))
    return (pres[n - 1], behind), (upper_part(partial), ahead)


def read_slot(source, refs, n):
    kind = source[0]
    if kind == "packed":
        ref, b = refs[source[1]], source[2]
        get = lambda c, i: ref[b, c, i]
    elif kind == "flat":
        ref = refs[source[1]]
        get = lambda c, i: ref[c, i]
    elif kind == "diff":
        ref, b, other = refs[source[1]], source[2], refs[source[3]]
        get = lambda c, i: ref[b, c, i] - other[c, i]
    else:
        pref, vref, lead = refs[source[1]], refs[source[2]], source[3]
        if lead:
            get = lambda c, i: pref[0, i] if c == 0 else vref[0, c - 1, i]
        else:
            get = lambda c, i: pref[i] if c == 0 else vref[c - 1, i]
    return [get(0, i) for i in range(n)], [[get(1 + c, i) for c in range(3)] for i in range(n)]


def write_messages(b, msgs, right_out, left_out):
    (p_last, behind), (share, ahead) = msgs
    right_out[2 * b] = p_last
    right_out[2 * b + 1] = behind
    left_out[2 * b] = share
    left_out[2 * b + 1] = ahead


def write_outputs(g_ref, st_ref, moved_ref, late, n, outs):
    cp_out, cv_out, rp_out, rv_out = outs

    def write(end_of, moved_of):
        for i in range(n):
            for c in range(4):
                relaxed = st_ref[0, c, i]
                resid = end_of(c, i) - relaxed
                error = resid if moved_of is None else resid + moved_of(c, i)
                if c == 0:
                    rp_out[0, i] = resid
                    cp_out[0, i] = relaxed + error
                else:
                    rv_out[0, c - 1, i] = resid
                    cv_out[0, c - 1, i] = relaxed + error

    @pl.when(g_ref[0] == 0)
    def _():
        write(lambda c, i: st_ref[1, c, i], None)

    @pl.when(g_ref[0] != 0)
    def _():
        write(lambda c, i: late[c][i], lambda c, i: moved_ref[1, c, i])


def pair_kernel(sizes, counts, sources, n_states, next_count, first, split, finish, handoff, *refs):
    states = refs[:n_states]
    k_ref, m_ref, c_ref, fl_ref, fr_ref = refs[n_states : n_states + 5]
    rest = refs[n_states + 5 :]
    if finish:
        g_ref, st_ref, moved_ref = rest[:3]
        outs = rest[3:]
    else:
        s_out = rest[0]
        outs = rest[1:]
    n = k_ref.shape[0]
    width = 2 * len(sizes)
    if first:
        next_mass, next_stiff, prev_stiff = fr_ref[width], fr_ref[width + 1], fl_ref[width]
    else:
        next_mass, next_stiff, prev_stiff = c_ref[0], c_ref[1], c_ref[2]
    zero = jnp.zeros_like(next_mass)
    results = []
    for b, (h, count) in enumerate(zip(sizes, counts)):
        pres, vel = read_slot(sources[b], states, n)
        lower = [fl_ref[2 * b]] + pres[:-1]
        vel1 = [[vel[i][c] + h * m_ref[i] * f for c, f in enumerate(forces(pres[i], lower[i]))]
                for i in range(n)]
        pres1 = [pres[i] - h * k_ref[i] * divergence(vel1[i], vel1[i + 1]) for i in range(n - 1)]
        below = [h * next_mass * f for f in forces(zero, pres[n - 1])]
        upper1 = fr_ref[2 * b] + upper_part(below)
        pres1.append(pres[n - 1] - h * k_ref[n - 1] * (0.25 * (lower_part(vel1[n - 1]) + upper1)))
        if count == 2:
            prev1 = fl_ref[2 * b + 1] - h * prev_stiff * (0.25 * upper_part(vel1[0]))
            next1 = fr_ref[2 * b + 1] - h * next_stiff * (0.25 * lower_part(below))
            lower = [prev1] + pres1[:-1]
            vel2 = [[vel1[i][c] + h * m_ref[i] * f for c, f in enumerate(forces(pres1[i], lower[i]))]
                    for i in range(n)]
            pres2 = [pres1[i] - h * k_ref[i] * divergence(vel2[i], vel2[i + 1]) for i in range(n - 1)]
            upper2 = upper1 + upper_part([h * next_mass * f for f in forces(next1, pres1[n - 1])])
            pres2.append(pres1[n - 1] - h * k_ref[n - 1] * (0.25 * (lower_part(vel2[n - 1]) + upper2)))
            pres1, vel1 = pres2, vel2
        if finish:
            late = [pres1] + [[vel1[i][c] for i in range(n)] for c in range(3)]
            write_outputs(g_ref, st_ref, moved_ref, late, n, outs)
            continue
        for i in range(n):
            s_out[b, 0, i] = pres1[i]
            for c in range(3):
                s_out[b, 1 + c, i] = vel1[i][c]
            if split and b == 0:
                split_out = outs[(2 if next_count else 0) + (1 if first else 0)]
                split_out[0, i] = pres1[i]
                for c in range(3):
                    split_out[1 + c, i] = vel1[i][c]
        if b < next_count:
            write_messages(b, messages(pres1, vel1, k_ref, m_ref, h), outs[0], outs[1])
        if handoff:
            results.append((pres1, vel1))
    at = 2 if next_count else 0
    if first:
        outs[at][0] = next_mass
        outs[at][1] = next_stiff
        outs[at][2] = prev_stiff
        at += 1
    if handoff:
        at += 1 if split else 0
        (p0, v0), (p1, v1) = results
        diff_p = [p1[i] - p0[i] for i in range(n)]
        diff_v = [[v1[i][c] - v0[i][c] for c in range(3)] for i in range(n)]
        for b, (pres, vel) in enumerate(((p0, v0), (diff_p, diff_v))):
            write_messages(b, messages(pres, vel, k_ref, m_ref, handoff[b]), outs[at], outs[at + 1])


def planes(count, like):
    return jax.ShapeDtypeStruct((count,) + like.shape[-2:], like.dtype)


def diagonal(x, by):
    spaces, groups = lax.axis_size("space"), lax.axis_size("tm")
    pairs = [
        (s * groups + c, (s + by) * groups + c + 1)
        for s in range(spaces)
        for c in range(groups - 1)
        if 0 <= s + by < spaces
    ]
    return lax.ppermute(x, ("space", "tm"), pairs)


def advance(states, sources, to_right, to_left, stiffness, inv_mass, consts, sizes, counts,
            next_count, split=False, finish=None, handoff=None, received=None):
    if received is None:
        from_left = from_behind(to_right, "space", 1)
        from_right = from_behind(to_left, "space", -1)
    else:
        from_left, from_right = received
    first = consts is None
    if first:
        consts = from_left
    n = stiffness.shape[0]
    args = list(states) + [stiffness, inv_mass, consts, from_left, from_right]
    vmem = pl.BlockSpec(memory_space=pltpu.VMEM)
    specs = [vmem] * len(args)
    if finish is not None:
        flat = jax.ShapeDtypeStruct((1,) + stiffness.shape, stiffness.dtype)
        vflat = jax.ShapeDtypeStruct((1, 3) + stiffness.shape, stiffness.dtype)
        outs = [flat, vflat, flat, vflat]
        args += list(finish)
        specs += [pl.BlockSpec(memory_space=pltpu.SMEM), vmem, vmem]
    else:
        outs = [jax.ShapeDtypeStruct((len(sizes), 4) + stiffness.shape, stiffness.dtype)]
        if next_count:
            outs += [planes(2 * next_count, stiffness), planes(2 * next_count, stiffness)]
        if first:
            outs.append(planes(3, stiffness))
        if split:
            outs.append(jax.ShapeDtypeStruct((4,) + stiffness.shape, stiffness.dtype))
        if handoff:
            outs += [planes(4, stiffness), planes(4, stiffness)]
    kernel = functools.partial(
        pair_kernel, tuple(sizes), tuple(counts), tuple(sources), len(states), next_count, first,
        split, finish is not None, handoff,
    )
    return pl.pallas_call(kernel, out_shape=tuple(outs), in_specs=specs)(*args)


def messages_kernel(sizes, sources, n_states, extras, *refs):
    states = refs[:n_states]
    k_ref, m_ref, right_out, left_out = refs[n_states:]
    n = k_ref.shape[0]
    for b, h in enumerate(sizes):
        pres, vel = read_slot(sources[b], states, n)
        write_messages(b, messages(pres, vel, k_ref, m_ref, h), right_out, left_out)
    if extras:
        width = 2 * len(sizes)
        right_out[width] = k_ref[n - 1]
        left_out[width] = m_ref[0]
        left_out[width + 1] = k_ref[0]


def first_messages(states, sources, stiffness, inv_mass, sizes, extras=False):
    width = 2 * len(sizes)
    kernel = functools.partial(messages_kernel, tuple(sizes), tuple(sources), len(states), extras)
    return pl.pallas_call(
        kernel,
        out_shape=(planes(width + (1 if extras else 0), stiffness), planes(width + (2 if extras else 0), stiffness)),
    )(*states, stiffness, inv_mass)


def coarse(carried, stiffness, inv_mass, consts):
    sources = (("flat", 0),)
    to_right, to_left = first_messages((carried,), sources, stiffness, inv_mass, (DT_COARSE,))
    (out,) = advance((carried,), sources, to_right, to_left, stiffness, inv_mass, consts,
                     (DT_COARSE,), (1,), 0)
    return out[0]


def on_device(
    guess_pressure, guess_velocity, initial_pressure, initial_velocity, stiffness, inv_mass
):
    fine_size = DT_COARSE / STEPS
    groups = lax.axis_size("tm")
    group = lax.axis_index("tm")
    assert stiffness.shape[0] >= 2 and STEPS % 2 == 0
    rounds = STEPS // 2
    fine2 = (fine_size, fine_size)

    inputs = (guess_pressure, guess_velocity, initial_pressure, initial_velocity)
    sources = (("input", 0, 1, True), ("input", 2, 3, False))
    to_right, to_left = first_messages(inputs, sources, stiffness, inv_mass, fine2, extras=True)
    state, to_right, to_left, consts = advance(
        inputs, sources, to_right, to_left, stiffness, inv_mass, None, fine2, (2, 2), 2,
    )
    packed = (("packed", 0, 0), ("packed", 0, 1))
    for repeat in range(1, rounds):
        count = 2 if repeat + 1 < rounds else 0
        last_round = repeat + 1 == rounds
        outs = advance(
            (state,), packed, to_right, to_left, stiffness, inv_mass, consts, fine2, (2, 2), count,
            split=last_round, handoff=(fine_size, DT_COARSE) if last_round else None,
        )
        state = outs[0]
        if count:
            to_right, to_left = outs[1], outs[2]
    relaxed, hand_right, hand_left = outs[-3], outs[-2], outs[-1]

    got = from_behind(relaxed, "tm", 1)
    received = (diagonal(hand_right, 1), diagonal(hand_left, -1))
    late_states = (got, state)
    late_sources = (("flat", 0), ("diff", 1, 1, 0))
    flag = jnp.reshape(group, (1,)).astype(jnp.int32)
    both = None
    late = None
    for repeat in range(rounds):
        count = 1 if repeat + 1 < rounds else 0
        if repeat == 0:
            sizes, counts, states, srcs = (fine_size, DT_COARSE), (2, 1), late_states, late_sources
        else:
            sizes, counts, states, srcs = (fine_size,), (2,), (late,), (("packed", 0, 0),)
        finish = (flag, state, both) if (groups == 2 and repeat + 1 == rounds) else None
        outs = advance(states, srcs, to_right, to_left, stiffness, inv_mass, consts, sizes, counts,
                       count, finish=finish, received=received if repeat == 0 else None)
        if finish is not None:
            return outs
        late = outs[0]
        if repeat == 0:
            both = late
        if count:
            to_right, to_left = outs[1], outs[2]

    end = jnp.where(group == 0, state[1], late[0])
    resid = end - relaxed
    error, carried = resid, resid
    for repeat in range(groups - 1):
        carried = from_behind(carried, "tm", 1)
        carried = coarse(carried, stiffness, inv_mass, consts)
        error = error + carried
    corrected = relaxed + error
    return (corrected[0][None], corrected[1:][None], resid[0][None], resid[1:][None])


def solution(mesh):
    placed = (
        P("tm", "space", None, None),
        P("tm", None, "space", None, None),
        P("space", None, None),
        P(None, "space", None, None),
        P("space", None, None),
        P("space", None, None),
    )
    return jax.shard_map(
        on_device,
        mesh=mesh,
        in_specs=placed,
        out_specs=(
            P("tm", "space", None, None),
            P("tm", None, "space", None, None),
            P("tm", "space", None, None),
            P("tm", None, "space", None, None),
        ),
        check_vma=False,
    )
```

```python
import functools

import jax
import jax.numpy as jnp
from jax import lax
from jax.experimental import pallas as pl
from jax.experimental.pallas import tpu as pltpu
from jax.sharding import PartitionSpec as P

STEPS = 4


DT_COARSE = 0.4


def from_behind(x, axis, by):
    size = lax.axis_size(axis)
    pairs = [(i, i + by) for i in range(size) if 0 <= i + by < size]
    return lax.ppermute(x, axis, pairs)


def roll(x, shift, axis):
    return pltpu.roll(x, shift % x.shape[axis], axis)


def nsum(values, offset, axis):
    return values + roll(values, offset, axis)


def forces(pressure, lower):
    combined = pressure + lower
    force_x = 0.25 * (nsum(nsum(lower, 1, 1), 1, 0) - nsum(nsum(pressure, 1, 1), 1, 0))
    across_z = nsum(combined, 1, 1)
    force_y = 0.25 * (roll(across_z, 1, 0) - across_z)
    across_y = nsum(combined, 1, 0)
    force_z = 0.25 * (roll(across_y, 1, 1) - across_y)
    return force_x, force_y, force_z


def divergence(v, u):
    diff_x = nsum(nsum(u[0] - v[0], -1, 1), -1, 0)
    sum_y = nsum(v[1] + u[1], -1, 1)
    diff_y = roll(sum_y, -1, 0) - sum_y
    sum_z = nsum(v[2] + u[2], -1, 0)
    diff_z = roll(sum_z, -1, 1) - sum_z
    return 0.25 * (diff_x + diff_y + diff_z)


def upper_part(u):
    diff_x = nsum(nsum(u[0], -1, 1), -1, 0)
    sum_y = nsum(u[1], -1, 1)
    diff_y = roll(sum_y, -1, 0) - sum_y
    sum_z = nsum(u[2], -1, 0)
    diff_z = roll(sum_z, -1, 1) - sum_z
    return diff_x + diff_y + diff_z


def lower_part(v):
    diff_x = nsum(nsum(-v[0], -1, 1), -1, 0)
    sum_y = nsum(v[1], -1, 1)
    diff_y = roll(sum_y, -1, 0) - sum_y
    sum_z = nsum(v[2], -1, 0)
    diff_z = roll(sum_z, -1, 1) - sum_z
    return diff_x + diff_y + diff_z


def outgoing(pressure_first, velocity_first, mass_first, step_size):
    f = forces(pressure_first, jnp.zeros_like(pressure_first))
    hm = step_size * mass_first
    return upper_part([velocity_first[c] + hm * f[c] for c in range(3)])


def messages(pres, vel, k_ref, m_ref, step_size):
    n = len(pres)
    last_node = [vel[n - 1][c] + step_size * m_ref[n - 1] * f
                 for c, f in enumerate(forces(pres[n - 1], pres[n - 2]))]
    behind = pres[n - 1] - step_size * k_ref[n - 1] * (0.25 * lower_part(last_node))
    f0 = forces(pres[0], jnp.zeros_like(pres[0]))
    partial = [vel[0][c] + step_size * m_ref[0] * f0[c] for c in range(3)]
    second = [vel[1][c] + step_size * m_ref[1] * f for c, f in enumerate(forces(pres[1], pres[0]))]
    ahead = pres[0] - step_size * k_ref[0] * (0.25 * (lower_part(partial) + upper_part(second)))
    return (pres[n - 1], behind), (upper_part(partial), ahead)


def read_slot(source, refs, n):
    kind = source[0]
    if kind == "packed":
        ref, b = refs[source[1]], source[2]
        get = lambda c, i: ref[b, c, i]
    elif kind == "flat":
        ref = refs[source[1]]
        get = lambda c, i: ref[c, i]
    elif kind == "diff":
        ref, b, other = refs[source[1]], source[2], refs[source[3]]
        get = lambda c, i: ref[b, c, i] - other[c, i]
    else:
        pref, vref, lead = refs[source[1]], refs[source[2]], source[3]
        if lead:
            get = lambda c, i: pref[0, i] if c == 0 else vref[0, c - 1, i]
        else:
            get = lambda c, i: pref[i] if c == 0 else vref[c - 1, i]
    return [get(0, i) for i in range(n)], [[get(1 + c, i) for c in range(3)] for i in range(n)]


def write_messages(b, msgs, right_out, left_out):
    (p_last, behind), (share, ahead) = msgs
    right_out[2 * b] = p_last
    right_out[2 * b + 1] = behind
    left_out[2 * b] = share
    left_out[2 * b + 1] = ahead


def write_outputs(g_ref, st_ref, moved_ref, late, n, outs):
    cp_out, cv_out, rp_out, rv_out = outs

    def write(end_of, moved_of):
        for i in range(n):
            for c in range(4):
                relaxed = st_ref[0, c, i]
                resid = end_of(c, i) - relaxed
                error = resid if moved_of is None else resid + moved_of(c, i)
                if c == 0:
                    rp_out[0, i] = resid
                    cp_out[0, i] = relaxed + error
                else:
                    rv_out[0, c - 1, i] = resid
                    cv_out[0, c - 1, i] = relaxed + error

    @pl.when(g_ref[0] == 0)
    def _():
        write(lambda c, i: st_ref[1, c, i], None)

    @pl.when(g_ref[0] != 0)
    def _():
        write(lambda c, i: late[c][i], lambda c, i: moved_ref[0, c, i])


def pair_kernel(sizes, counts, sources, n_states, next_count, first, split, finish, handoff, offset,
                *refs):
    states = refs[:n_states]
    k_ref, m_ref, c_ref, fl_ref, fr_ref = refs[n_states : n_states + 5]
    rest = refs[n_states + 5 :]
    if finish:
        g_ref, st_ref, moved_ref = rest[:3]
        outs = rest[3:]
    else:
        s_out = rest[0]
        outs = rest[1:]
    n = k_ref.shape[0]
    width = 2 * len(sizes)
    if first:
        next_mass, next_stiff, prev_stiff = fr_ref[width], fr_ref[width + 1], fl_ref[width]
    else:
        next_mass, next_stiff, prev_stiff = c_ref[0], c_ref[1], c_ref[2]
    zero = jnp.zeros_like(next_mass)
    results = []
    for b, (h, count) in enumerate(zip(sizes, counts)):
        pres, vel = read_slot(sources[b], states, n)
        m = b + offset
        lower = [fl_ref[2 * m]] + pres[:-1]
        vel1 = [[vel[i][c] + h * m_ref[i] * f for c, f in enumerate(forces(pres[i], lower[i]))]
                for i in range(n)]
        pres1 = [pres[i] - h * k_ref[i] * divergence(vel1[i], vel1[i + 1]) for i in range(n - 1)]
        below = [h * next_mass * f for f in forces(zero, pres[n - 1])]
        upper1 = fr_ref[2 * m] + upper_part(below)
        pres1.append(pres[n - 1] - h * k_ref[n - 1] * (0.25 * (lower_part(vel1[n - 1]) + upper1)))
        if count == 2:
            prev1 = fl_ref[2 * m + 1] - h * prev_stiff * (0.25 * upper_part(vel1[0]))
            next1 = fr_ref[2 * m + 1] - h * next_stiff * (0.25 * lower_part(below))
            lower = [prev1] + pres1[:-1]
            vel2 = [[vel1[i][c] + h * m_ref[i] * f for c, f in enumerate(forces(pres1[i], lower[i]))]
                    for i in range(n)]
            pres2 = [pres1[i] - h * k_ref[i] * divergence(vel2[i], vel2[i + 1]) for i in range(n - 1)]
            upper2 = upper1 + upper_part([h * next_mass * f for f in forces(next1, pres1[n - 1])])
            pres2.append(pres1[n - 1] - h * k_ref[n - 1] * (0.25 * (lower_part(vel2[n - 1]) + upper2)))
            pres1, vel1 = pres2, vel2
        if finish:
            late = [pres1] + [[vel1[i][c] for i in range(n)] for c in range(3)]
            write_outputs(g_ref, st_ref, moved_ref, late, n, outs)
            continue
        for i in range(n):
            s_out[b, 0, i] = pres1[i]
            for c in range(3):
                s_out[b, 1 + c, i] = vel1[i][c]
            if split and b == 0:
                split_out = outs[(2 if next_count else 0) + (1 if first else 0)]
                split_out[0, i] = pres1[i]
                for c in range(3):
                    split_out[1 + c, i] = vel1[i][c]
        if b < next_count:
            write_messages(b, messages(pres1, vel1, k_ref, m_ref, h), outs[0], outs[1])
        if handoff:
            results.append((pres1, vel1))
    at = 2 if next_count else 0
    if first:
        outs[at][0] = next_mass
        outs[at][1] = next_stiff
        outs[at][2] = prev_stiff
        at += 1
    if handoff:
        at += 1 if split else 0
        (p0, v0), (p1, v1) = results
        diff_p = [p1[i] - p0[i] for i in range(n)]
        diff_v = [[v1[i][c] - v0[i][c] for c in range(3)] for i in range(n)]
        for b, (pres, vel) in enumerate(((p0, v0), (diff_p, diff_v))):
            write_messages(b, messages(pres, vel, k_ref, m_ref, handoff[b]), outs[at], outs[at + 1])


def planes(count, like):
    return jax.ShapeDtypeStruct((count,) + like.shape[-2:], like.dtype)


def diagonal(x, by):
    spaces, groups = lax.axis_size("space"), lax.axis_size("tm")
    pairs = [
        (s * groups + c, (s + by) * groups + c + 1)
        for s in range(spaces)
        for c in range(groups - 1)
        if 0 <= s + by < spaces
    ]
    return lax.ppermute(x, ("space", "tm"), pairs)


def advance(states, sources, to_right, to_left, stiffness, inv_mass, consts, sizes, counts,
            next_count, split=False, finish=None, handoff=None, received=None, offset=0):
    if received is None:
        from_left = from_behind(to_right, "space", 1)
        from_right = from_behind(to_left, "space", -1)
    else:
        from_left, from_right = received
    first = consts is None
    if first:
        consts = from_left
    n = stiffness.shape[0]
    args = list(states) + [stiffness, inv_mass, consts, from_left, from_right]
    vmem = pl.BlockSpec(memory_space=pltpu.VMEM)
    specs = [vmem] * len(args)
    if finish is not None:
        flat = jax.ShapeDtypeStruct((1,) + stiffness.shape, stiffness.dtype)
        vflat = jax.ShapeDtypeStruct((1, 3) + stiffness.shape, stiffness.dtype)
        outs = [flat, vflat, flat, vflat]
        args += list(finish)
        specs += [pl.BlockSpec(memory_space=pltpu.SMEM), vmem, vmem]
    else:
        outs = [jax.ShapeDtypeStruct((len(sizes), 4) + stiffness.shape, stiffness.dtype)]
        if next_count:
            outs += [planes(2 * next_count, stiffness), planes(2 * next_count, stiffness)]
        if first:
            outs.append(planes(3, stiffness))
        if split:
            outs.append(jax.ShapeDtypeStruct((4,) + stiffness.shape, stiffness.dtype))
        if handoff:
            outs += [planes(4, stiffness), planes(4, stiffness)]
    kernel = functools.partial(
        pair_kernel, tuple(sizes), tuple(counts), tuple(sources), len(states), next_count, first,
        split, finish is not None, handoff, offset,
    )
    return pl.pallas_call(kernel, out_shape=tuple(outs), in_specs=specs)(*args)


def messages_kernel(sizes, sources, n_states, extras, *refs):
    states = refs[:n_states]
    k_ref, m_ref, right_out, left_out = refs[n_states:]
    n = k_ref.shape[0]
    for b, h in enumerate(sizes):
        pres, vel = read_slot(sources[b], states, n)
        write_messages(b, messages(pres, vel, k_ref, m_ref, h), right_out, left_out)
    if extras:
        width = 2 * len(sizes)
        right_out[width] = k_ref[n - 1]
        left_out[width] = m_ref[0]
        left_out[width + 1] = k_ref[0]


def first_messages(states, sources, stiffness, inv_mass, sizes, extras=False):
    width = 2 * len(sizes)
    kernel = functools.partial(messages_kernel, tuple(sizes), tuple(sources), len(states), extras)
    return pl.pallas_call(
        kernel,
        out_shape=(planes(width + (1 if extras else 0), stiffness), planes(width + (2 if extras else 0), stiffness)),
    )(*states, stiffness, inv_mass)


def coarse(carried, stiffness, inv_mass, consts):
    sources = (("flat", 0),)
    to_right, to_left = first_messages((carried,), sources, stiffness, inv_mass, (DT_COARSE,))
    (out,) = advance((carried,), sources, to_right, to_left, stiffness, inv_mass, consts,
                     (DT_COARSE,), (1,), 0)
    return out[0]


def on_device(
    guess_pressure, guess_velocity, initial_pressure, initial_velocity, stiffness, inv_mass
):
    fine_size = DT_COARSE / STEPS
    groups = lax.axis_size("tm")
    group = lax.axis_index("tm")
    assert stiffness.shape[0] >= 2 and STEPS % 2 == 0
    rounds = STEPS // 2
    fine2 = (fine_size, fine_size)

    inputs = (guess_pressure, guess_velocity, initial_pressure, initial_velocity)
    sources = (("input", 0, 1, True), ("input", 2, 3, False))
    to_right, to_left = first_messages(inputs, sources, stiffness, inv_mass, fine2, extras=True)
    state, to_right, to_left, consts = advance(
        inputs, sources, to_right, to_left, stiffness, inv_mass, None, fine2, (2, 2), 2,
    )
    packed = (("packed", 0, 0), ("packed", 0, 1))
    for repeat in range(1, rounds):
        count = 2 if repeat + 1 < rounds else 0
        last_round = repeat + 1 == rounds
        outs = advance(
            (state,), packed, to_right, to_left, stiffness, inv_mass, consts, fine2, (2, 2), count,
            split=last_round, handoff=(fine_size, DT_COARSE) if last_round else None,
        )
        state = outs[0]
        if count:
            to_right, to_left = outs[1], outs[2]
    relaxed, hand_right, hand_left = outs[-3], outs[-2], outs[-1]

    got = from_behind(relaxed, "tm", 1)
    received = (diagonal(hand_right, 1), diagonal(hand_left, -1))
    late_states = (got, state)
    late_sources = (("flat", 0), ("diff", 1, 1, 0))
    flag = jnp.reshape(group, (1,)).astype(jnp.int32)
    (moved,) = advance(late_states, (late_sources[1],), None, None, stiffness, inv_mass, consts,
                       (DT_COARSE,), (1,), 0, received=received, offset=1)
    late = None
    for repeat in range(rounds):
        count = 1 if repeat + 1 < rounds else 0
        if repeat == 0:
            states, srcs = late_states, late_sources[:1]
        else:
            states, srcs = (late,), (("packed", 0, 0),)
        finish = (flag, state, moved) if (groups == 2 and repeat + 1 == rounds) else None
        outs = advance(states, srcs, to_right, to_left, stiffness, inv_mass, consts, (fine_size,),
                       (2,), count, finish=finish, received=received if repeat == 0 else None)
        if finish is not None:
            return outs
        late = outs[0]
        if count:
            to_right, to_left = outs[1], outs[2]

    end = jnp.where(group == 0, state[1], late[0])
    resid = end - relaxed
    error, carried = resid, resid
    for repeat in range(groups - 1):
        carried = from_behind(carried, "tm", 1)
        carried = coarse(carried, stiffness, inv_mass, consts)
        error = error + carried
    corrected = relaxed + error
    return (corrected[0][None], corrected[1:][None], resid[0][None], resid[1:][None])


def solution(mesh):
    placed = (
        P("tm", "space", None, None),
        P("tm", None, "space", None, None),
        P("space", None, None),
        P(None, "space", None, None),
        P("space", None, None),
        P("space", None, None),
    )
    return jax.shard_map(
        on_device,
        mesh=mesh,
        in_specs=placed,
        out_specs=(
            P("tm", "space", None, None),
            P("tm", None, "space", None, None),
            P("tm", "space", None, None),
            P("tm", None, "space", None, None),
        ),
        check_vma=False,
    )
```

```python
import functools

import jax
import jax.numpy as jnp
from jax import lax
from jax.experimental import pallas as pl
from jax.experimental.pallas import tpu as pltpu
from jax.sharding import PartitionSpec as P

STEPS = 4


DT_COARSE = 0.4


def from_behind(x, axis, by):
    size = lax.axis_size(axis)
    pairs = [(i, i + by) for i in range(size) if 0 <= i + by < size]
    return lax.ppermute(x, axis, pairs)


def roll(x, shift, axis):
    return pltpu.roll(x, shift % x.shape[axis], axis)


def nsum(values, offset, axis):
    return values + roll(values, offset, axis)


def forces(pressure, lower):
    combined = pressure + lower
    force_x = 0.25 * nsum(nsum(lower - pressure, 1, 1), 1, 0)
    across_z = nsum(combined, 1, 1)
    force_y = 0.25 * (roll(across_z, 1, 0) - across_z)
    across_y = nsum(combined, 1, 0)
    force_z = 0.25 * (roll(across_y, 1, 1) - across_y)
    return force_x, force_y, force_z


def divergence(v, u):
    diff_x = nsum(nsum(u[0] - v[0], -1, 1), -1, 0)
    sum_y = nsum(v[1] + u[1], -1, 1)
    diff_y = roll(sum_y, -1, 0) - sum_y
    sum_z = nsum(v[2] + u[2], -1, 0)
    diff_z = roll(sum_z, -1, 1) - sum_z
    return 0.25 * (diff_x + diff_y + diff_z)


def upper_part(u):
    diff_x = nsum(nsum(u[0], -1, 1), -1, 0)
    sum_y = nsum(u[1], -1, 1)
    diff_y = roll(sum_y, -1, 0) - sum_y
    sum_z = nsum(u[2], -1, 0)
    diff_z = roll(sum_z, -1, 1) - sum_z
    return diff_x + diff_y + diff_z


def lower_part(v):
    diff_x = nsum(nsum(-v[0], -1, 1), -1, 0)
    sum_y = nsum(v[1], -1, 1)
    diff_y = roll(sum_y, -1, 0) - sum_y
    sum_z = nsum(v[2], -1, 0)
    diff_z = roll(sum_z, -1, 1) - sum_z
    return diff_x + diff_y + diff_z


def outgoing(pressure_first, velocity_first, mass_first, step_size):
    f = forces(pressure_first, jnp.zeros_like(pressure_first))
    hm = step_size * mass_first
    return upper_part([velocity_first[c] + hm * f[c] for c in range(3)])


def messages(pres, vel, k_ref, m_ref, step_size):
    n = len(pres)
    last_node = [vel[n - 1][c] + step_size * m_ref[n - 1] * f
                 for c, f in enumerate(forces(pres[n - 1], pres[n - 2]))]
    behind = pres[n - 1] - step_size * k_ref[n - 1] * (0.25 * lower_part(last_node))
    f0 = forces(pres[0], jnp.zeros_like(pres[0]))
    partial = [vel[0][c] + step_size * m_ref[0] * f0[c] for c in range(3)]
    second = [vel[1][c] + step_size * m_ref[1] * f for c, f in enumerate(forces(pres[1], pres[0]))]
    ahead = pres[0] - step_size * k_ref[0] * (0.25 * (lower_part(partial) + upper_part(second)))
    return (pres[n - 1], behind), (upper_part(partial), ahead)


def read_slot(source, refs, n):
    kind = source[0]
    if kind == "packed":
        ref, b = refs[source[1]], source[2]
        get = lambda c, i: ref[b, c, i]
    elif kind == "flat":
        ref = refs[source[1]]
        get = lambda c, i: ref[c, i]
    elif kind == "diff":
        ref, b, other = refs[source[1]], source[2], refs[source[3]]
        get = lambda c, i: ref[b, c, i] - other[c, i]
    else:
        pref, vref, lead = refs[source[1]], refs[source[2]], source[3]
        if lead:
            get = lambda c, i: pref[0, i] if c == 0 else vref[0, c - 1, i]
        else:
            get = lambda c, i: pref[i] if c == 0 else vref[c - 1, i]
    return [get(0, i) for i in range(n)], [[get(1 + c, i) for c in range(3)] for i in range(n)]


def write_messages(b, msgs, right_out, left_out):
    (p_last, behind), (share, ahead) = msgs
    right_out[2 * b] = p_last
    right_out[2 * b + 1] = behind
    left_out[2 * b] = share
    left_out[2 * b + 1] = ahead


def write_outputs(g_ref, st_ref, moved_ref, late, n, outs):
    cp_out, cv_out, rp_out, rv_out = outs

    def write(end_of, moved_of):
        for i in range(n):
            for c in range(4):
                relaxed = st_ref[0, c, i]
                resid = end_of(c, i) - relaxed
                error = resid if moved_of is None else resid + moved_of(c, i)
                if c == 0:
                    rp_out[0, i] = resid
                    cp_out[0, i] = relaxed + error
                else:
                    rv_out[0, c - 1, i] = resid
                    cv_out[0, c - 1, i] = relaxed + error

    @pl.when(g_ref[0] == 0)
    def _():
        write(lambda c, i: st_ref[1, c, i], None)

    @pl.when(g_ref[0] != 0)
    def _():
        write(lambda c, i: late[c][i], lambda c, i: moved_ref[0, c, i])


def pair_kernel(sizes, counts, sources, n_states, next_count, first, split, finish, handoff, offset,
                *refs):
    states = refs[:n_states]
    k_ref, m_ref, c_ref, fl_ref, fr_ref = refs[n_states : n_states + 5]
    rest = refs[n_states + 5 :]
    if finish:
        g_ref, st_ref, moved_ref = rest[:3]
        outs = rest[3:]
    else:
        s_out = rest[0]
        outs = rest[1:]
    n = k_ref.shape[0]
    width = 2 * len(sizes)
    if first:
        next_mass, next_stiff, prev_stiff = fr_ref[width], fr_ref[width + 1], fl_ref[width]
    else:
        next_mass, next_stiff, prev_stiff = c_ref[0], c_ref[1], c_ref[2]
    zero = jnp.zeros_like(next_mass)
    results = []
    for b, (h, count) in enumerate(zip(sizes, counts)):
        pres, vel = read_slot(sources[b], states, n)
        m = b + offset
        lower = [fl_ref[2 * m]] + pres[:-1]
        vel1 = [[vel[i][c] + h * m_ref[i] * f for c, f in enumerate(forces(pres[i], lower[i]))]
                for i in range(n)]
        pres1 = [pres[i] - h * k_ref[i] * divergence(vel1[i], vel1[i + 1]) for i in range(n - 1)]
        below = [h * next_mass * f for f in forces(zero, pres[n - 1])]
        upper1 = fr_ref[2 * m] + upper_part(below)
        pres1.append(pres[n - 1] - h * k_ref[n - 1] * (0.25 * (lower_part(vel1[n - 1]) + upper1)))
        if count == 2:
            prev1 = fl_ref[2 * m + 1] - h * prev_stiff * (0.25 * upper_part(vel1[0]))
            next1 = fr_ref[2 * m + 1] - h * next_stiff * (0.25 * lower_part(below))
            lower = [prev1] + pres1[:-1]
            vel2 = [[vel1[i][c] + h * m_ref[i] * f for c, f in enumerate(forces(pres1[i], lower[i]))]
                    for i in range(n)]
            pres2 = [pres1[i] - h * k_ref[i] * divergence(vel2[i], vel2[i + 1]) for i in range(n - 1)]
            upper2 = upper1 + upper_part([h * next_mass * f for f in forces(next1, pres1[n - 1])])
            pres2.append(pres1[n - 1] - h * k_ref[n - 1] * (0.25 * (lower_part(vel2[n - 1]) + upper2)))
            pres1, vel1 = pres2, vel2
        if finish:
            late = [pres1] + [[vel1[i][c] for i in range(n)] for c in range(3)]
            write_outputs(g_ref, st_ref, moved_ref, late, n, outs)
            continue
        for i in range(n):
            s_out[b, 0, i] = pres1[i]
            for c in range(3):
                s_out[b, 1 + c, i] = vel1[i][c]
            if split and b == 0:
                split_out = outs[(2 if next_count else 0) + (1 if first else 0)]
                split_out[0, i] = pres1[i]
                for c in range(3):
                    split_out[1 + c, i] = vel1[i][c]
        if b < next_count:
            write_messages(b, messages(pres1, vel1, k_ref, m_ref, h), outs[0], outs[1])
        if handoff:
            results.append((pres1, vel1))
    at = 2 if next_count else 0
    if first:
        outs[at][0] = next_mass
        outs[at][1] = next_stiff
        outs[at][2] = prev_stiff
        at += 1
    if handoff:
        at += 1 if split else 0
        (p0, v0), (p1, v1) = results
        diff_p = [p1[i] - p0[i] for i in range(n)]
        diff_v = [[v1[i][c] - v0[i][c] for c in range(3)] for i in range(n)]
        for b, (pres, vel) in enumerate(((p0, v0), (diff_p, diff_v))):
            write_messages(b, messages(pres, vel, k_ref, m_ref, handoff[b]), outs[at], outs[at + 1])


def planes(count, like):
    return jax.ShapeDtypeStruct((count,) + like.shape[-2:], like.dtype)


def diagonal(x, by):
    spaces, groups = lax.axis_size("space"), lax.axis_size("tm")
    pairs = [
        (s * groups + c, (s + by) * groups + c + 1)
        for s in range(spaces)
        for c in range(groups - 1)
        if 0 <= s + by < spaces
    ]
    return lax.ppermute(x, ("space", "tm"), pairs)


def advance(states, sources, to_right, to_left, stiffness, inv_mass, consts, sizes, counts,
            next_count, split=False, finish=None, handoff=None, received=None, offset=0):
    if received is None:
        from_left = from_behind(to_right, "space", 1)
        from_right = from_behind(to_left, "space", -1)
    else:
        from_left, from_right = received
    first = consts is None
    if first:
        consts = from_left
    n = stiffness.shape[0]
    args = list(states) + [stiffness, inv_mass, consts, from_left, from_right]
    vmem = pl.BlockSpec(memory_space=pltpu.VMEM)
    specs = [vmem] * len(args)
    if finish is not None:
        flat = jax.ShapeDtypeStruct((1,) + stiffness.shape, stiffness.dtype)
        vflat = jax.ShapeDtypeStruct((1, 3) + stiffness.shape, stiffness.dtype)
        outs = [flat, vflat, flat, vflat]
        args += list(finish)
        specs += [pl.BlockSpec(memory_space=pltpu.SMEM), vmem, vmem]
    else:
        outs = [jax.ShapeDtypeStruct((len(sizes), 4) + stiffness.shape, stiffness.dtype)]
        if next_count:
            outs += [planes(2 * next_count, stiffness), planes(2 * next_count, stiffness)]
        if first:
            outs.append(planes(3, stiffness))
        if split:
            outs.append(jax.ShapeDtypeStruct((4,) + stiffness.shape, stiffness.dtype))
        if handoff:
            outs += [planes(4, stiffness), planes(4, stiffness)]
    kernel = functools.partial(
        pair_kernel, tuple(sizes), tuple(counts), tuple(sources), len(states), next_count, first,
        split, finish is not None, handoff, offset,
    )
    return pl.pallas_call(kernel, out_shape=tuple(outs), in_specs=specs)(*args)


def messages_kernel(sizes, sources, n_states, extras, *refs):
    states = refs[:n_states]
    k_ref, m_ref, right_out, left_out = refs[n_states:]
    n = k_ref.shape[0]
    for b, h in enumerate(sizes):
        pres, vel = read_slot(sources[b], states, n)
        write_messages(b, messages(pres, vel, k_ref, m_ref, h), right_out, left_out)
    if extras:
        width = 2 * len(sizes)
        right_out[width] = k_ref[n - 1]
        left_out[width] = m_ref[0]
        left_out[width + 1] = k_ref[0]


def first_messages(states, sources, stiffness, inv_mass, sizes, extras=False):
    width = 2 * len(sizes)
    kernel = functools.partial(messages_kernel, tuple(sizes), tuple(sources), len(states), extras)
    return pl.pallas_call(
        kernel,
        out_shape=(planes(width + (1 if extras else 0), stiffness), planes(width + (2 if extras else 0), stiffness)),
    )(*states, stiffness, inv_mass)


def coarse(carried, stiffness, inv_mass, consts):
    sources = (("flat", 0),)
    to_right, to_left = first_messages((carried,), sources, stiffness, inv_mass, (DT_COARSE,))
    (out,) = advance((carried,), sources, to_right, to_left, stiffness, inv_mass, consts,
                     (DT_COARSE,), (1,), 0)
    return out[0]


def on_device(
    guess_pressure, guess_velocity, initial_pressure, initial_velocity, stiffness, inv_mass
):
    fine_size = DT_COARSE / STEPS
    groups = lax.axis_size("tm")
    group = lax.axis_index("tm")
    assert stiffness.shape[0] >= 2 and STEPS % 2 == 0
    rounds = STEPS // 2
    fine2 = (fine_size, fine_size)

    inputs = (guess_pressure, guess_velocity, initial_pressure, initial_velocity)
    sources = (("input", 0, 1, True), ("input", 2, 3, False))
    to_right, to_left = first_messages(inputs, sources, stiffness, inv_mass, fine2, extras=True)
    state, to_right, to_left, consts = advance(
        inputs, sources, to_right, to_left, stiffness, inv_mass, None, fine2, (2, 2), 2,
    )
    packed = (("packed", 0, 0), ("packed", 0, 1))
    for repeat in range(1, rounds):
        count = 2 if repeat + 1 < rounds else 0
        last_round = repeat + 1 == rounds
        outs = advance(
            (state,), packed, to_right, to_left, stiffness, inv_mass, consts, fine2, (2, 2), count,
            split=last_round, handoff=(fine_size, DT_COARSE) if last_round else None,
        )
        state = outs[0]
        if count:
            to_right, to_left = outs[1], outs[2]
    relaxed, hand_right, hand_left = outs[-3], outs[-2], outs[-1]

    got = from_behind(relaxed, "tm", 1)
    received = (diagonal(hand_right, 1), diagonal(hand_left, -1))
    late_states = (got, state)
    late_sources = (("flat", 0), ("diff", 1, 1, 0))
    flag = jnp.reshape(group, (1,)).astype(jnp.int32)
    (moved,) = advance(late_states, (late_sources[1],), None, None, stiffness, inv_mass, consts,
                       (DT_COARSE,), (1,), 0, received=received, offset=1)
    late = None
    for repeat in range(rounds):
        count = 1 if repeat + 1 < rounds else 0
        if repeat == 0:
            states, srcs = late_states, late_sources[:1]
        else:
            states, srcs = (late,), (("packed", 0, 0),)
        finish = (flag, state, moved) if (groups == 2 and repeat + 1 == rounds) else None
        outs = advance(states, srcs, to_right, to_left, stiffness, inv_mass, consts, (fine_size,),
                       (2,), count, finish=finish, received=received if repeat == 0 else None)
        if finish is not None:
            return outs
        late = outs[0]
        if count:
            to_right, to_left = outs[1], outs[2]

    end = jnp.where(group == 0, state[1], late[0])
    resid = end - relaxed
    error, carried = resid, resid
    for repeat in range(groups - 1):
        carried = from_behind(carried, "tm", 1)
        carried = coarse(carried, stiffness, inv_mass, consts)
        error = error + carried
    corrected = relaxed + error
    return (corrected[0][None], corrected[1:][None], resid[0][None], resid[1:][None])


def solution(mesh):
    placed = (
        P("tm", "space", None, None),
        P("tm", None, "space", None, None),
        P("space", None, None),
        P(None, "space", None, None),
        P("space", None, None),
        P("space", None, None),
    )
    return jax.shard_map(
        on_device,
        mesh=mesh,
        in_specs=placed,
        out_specs=(
            P("tm", "space", None, None),
            P("tm", None, "space", None, None),
            P("tm", "space", None, None),
            P("tm", None, "space", None, None),
        ),
        check_vma=False,
    )
```

```python
import functools

import jax
import jax.numpy as jnp
from jax import lax
from jax.experimental import pallas as pl
from jax.experimental.pallas import tpu as pltpu
from jax.sharding import PartitionSpec as P

STEPS = 4


DT_COARSE = 0.4

PARAMS = pltpu.CompilerParams()


def from_behind(x, axis, by):
    size = lax.axis_size(axis)
    pairs = [(i, i + by) for i in range(size) if 0 <= i + by < size]
    return lax.ppermute(x, axis, pairs)


def roll(x, shift, axis):
    return pltpu.roll(x, shift % x.shape[axis], axis)


def nsum(values, offset, axis):
    return values + roll(values, offset, axis)


def forces(pressure, lower):
    combined = pressure + lower
    force_x = 0.25 * (nsum(nsum(lower, 1, 1), 1, 0) - nsum(nsum(pressure, 1, 1), 1, 0))
    across_z = nsum(combined, 1, 1)
    force_y = 0.25 * (roll(across_z, 1, 0) - across_z)
    across_y = nsum(combined, 1, 0)
    force_z = 0.25 * (roll(across_y, 1, 1) - across_y)
    return force_x, force_y, force_z


def divergence(v, u):
    diff_x = nsum(nsum(u[0] - v[0], -1, 1), -1, 0)
    sum_y = nsum(v[1] + u[1], -1, 1)
    diff_y = roll(sum_y, -1, 0) - sum_y
    sum_z = nsum(v[2] + u[2], -1, 0)
    diff_z = roll(sum_z, -1, 1) - sum_z
    return 0.25 * (diff_x + diff_y + diff_z)


def upper_part(u):
    diff_x = nsum(nsum(u[0], -1, 1), -1, 0)
    sum_y = nsum(u[1], -1, 1)
    diff_y = roll(sum_y, -1, 0) - sum_y
    sum_z = nsum(u[2], -1, 0)
    diff_z = roll(sum_z, -1, 1) - sum_z
    return diff_x + diff_y + diff_z


def lower_part(v):
    diff_x = nsum(nsum(-v[0], -1, 1), -1, 0)
    sum_y = nsum(v[1], -1, 1)
    diff_y = roll(sum_y, -1, 0) - sum_y
    sum_z = nsum(v[2], -1, 0)
    diff_z = roll(sum_z, -1, 1) - sum_z
    return diff_x + diff_y + diff_z


def outgoing(pressure_first, velocity_first, mass_first, step_size):
    f = forces(pressure_first, jnp.zeros_like(pressure_first))
    hm = step_size * mass_first
    return upper_part([velocity_first[c] + hm * f[c] for c in range(3)])


def messages(pres, vel, k_ref, m_ref, step_size):
    n = len(pres)
    last_node = [vel[n - 1][c] + step_size * m_ref[n - 1] * f
                 for c, f in enumerate(forces(pres[n - 1], pres[n - 2]))]
    behind = pres[n - 1] - step_size * k_ref[n - 1] * (0.25 * lower_part(last_node))
    f0 = forces(pres[0], jnp.zeros_like(pres[0]))
    partial = [vel[0][c] + step_size * m_ref[0] * f0[c] for c in range(3)]
    second = [vel[1][c] + step_size * m_ref[1] * f for c, f in enumerate(forces(pres[1], pres[0]))]
    ahead = pres[0] - step_size * k_ref[0] * (0.25 * (lower_part(partial) + upper_part(second)))
    return (pres[n - 1], behind), (upper_part(partial), ahead)


def read_slot(source, refs, n):
    kind = source[0]
    if kind == "packed":
        ref, b = refs[source[1]], source[2]
        get = lambda c, i: ref[b, c, i]
    elif kind == "flat":
        ref = refs[source[1]]
        get = lambda c, i: ref[c, i]
    elif kind == "diff":
        ref, b, other = refs[source[1]], source[2], refs[source[3]]
        get = lambda c, i: ref[b, c, i] - other[c, i]
    else:
        pref, vref, lead = refs[source[1]], refs[source[2]], source[3]
        if lead:
            get = lambda c, i: pref[0, i] if c == 0 else vref[0, c - 1, i]
        else:
            get = lambda c, i: pref[i] if c == 0 else vref[c - 1, i]
    return [get(0, i) for i in range(n)], [[get(1 + c, i) for c in range(3)] for i in range(n)]


def write_messages(b, msgs, right_out, left_out):
    (p_last, behind), (share, ahead) = msgs
    right_out[2 * b] = p_last
    right_out[2 * b + 1] = behind
    left_out[2 * b] = share
    left_out[2 * b + 1] = ahead


def write_outputs(g_ref, st_ref, moved_ref, late, n, outs):
    cp_out, cv_out, rp_out, rv_out = outs

    def write(end_of, moved_of):
        for i in range(n):
            for c in range(4):
                relaxed = st_ref[0, c, i]
                resid = end_of(c, i) - relaxed
                error = resid if moved_of is None else resid + moved_of(c, i)
                if c == 0:
                    rp_out[0, i] = resid
                    cp_out[0, i] = relaxed + error
                else:
                    rv_out[0, c - 1, i] = resid
                    cv_out[0, c - 1, i] = relaxed + error

    @pl.when(g_ref[0] == 0)
    def _():
        write(lambda c, i: st_ref[1, c, i], None)

    @pl.when(g_ref[0] != 0)
    def _():
        write(lambda c, i: late[c][i], lambda c, i: moved_ref[0, c, i])


def pair_kernel(sizes, counts, sources, n_states, next_count, first, split, finish, handoff, offset,
                *refs):
    states = refs[:n_states]
    k_ref, m_ref, c_ref, fl_ref, fr_ref = refs[n_states : n_states + 5]
    rest = refs[n_states + 5 :]
    if finish:
        g_ref, st_ref, moved_ref = rest[:3]
        outs = rest[3:]
    else:
        s_out = rest[0]
        outs = rest[1:]
    n = k_ref.shape[0]
    width = 2 * len(sizes)
    if first:
        next_mass, next_stiff, prev_stiff = fr_ref[width], fr_ref[width + 1], fl_ref[width]
    else:
        next_mass, next_stiff, prev_stiff = c_ref[0], c_ref[1], c_ref[2]
    zero = jnp.zeros_like(next_mass)
    results = []
    for b, (h, count) in enumerate(zip(sizes, counts)):
        pres, vel = read_slot(sources[b], states, n)
        m = b + offset
        lower = [fl_ref[2 * m]] + pres[:-1]
        vel1 = [[vel[i][c] + h * m_ref[i] * f for c, f in enumerate(forces(pres[i], lower[i]))]
                for i in range(n)]
        pres1 = [pres[i] - h * k_ref[i] * divergence(vel1[i], vel1[i + 1]) for i in range(n - 1)]
        below = [h * next_mass * f for f in forces(zero, pres[n - 1])]
        upper1 = fr_ref[2 * m] + upper_part(below)
        pres1.append(pres[n - 1] - h * k_ref[n - 1] * (0.25 * (lower_part(vel1[n - 1]) + upper1)))
        if count == 2:
            prev1 = fl_ref[2 * m + 1] - h * prev_stiff * (0.25 * upper_part(vel1[0]))
            next1 = fr_ref[2 * m + 1] - h * next_stiff * (0.25 * lower_part(below))
            lower = [prev1] + pres1[:-1]
            vel2 = [[vel1[i][c] + h * m_ref[i] * f for c, f in enumerate(forces(pres1[i], lower[i]))]
                    for i in range(n)]
            pres2 = [pres1[i] - h * k_ref[i] * divergence(vel2[i], vel2[i + 1]) for i in range(n - 1)]
            upper2 = upper1 + upper_part([h * next_mass * f for f in forces(next1, pres1[n - 1])])
            pres2.append(pres1[n - 1] - h * k_ref[n - 1] * (0.25 * (lower_part(vel2[n - 1]) + upper2)))
            pres1, vel1 = pres2, vel2
        if finish:
            late = [pres1] + [[vel1[i][c] for i in range(n)] for c in range(3)]
            write_outputs(g_ref, st_ref, moved_ref, late, n, outs)
            continue
        for i in range(n):
            s_out[b, 0, i] = pres1[i]
            for c in range(3):
                s_out[b, 1 + c, i] = vel1[i][c]
            if split and b == 0:
                split_out = outs[(2 if next_count else 0) + (1 if first else 0)]
                split_out[0, i] = pres1[i]
                for c in range(3):
                    split_out[1 + c, i] = vel1[i][c]
        if b < next_count:
            write_messages(b, messages(pres1, vel1, k_ref, m_ref, h), outs[0], outs[1])
        if handoff:
            results.append((pres1, vel1))
    at = 2 if next_count else 0
    if first:
        outs[at][0] = next_mass
        outs[at][1] = next_stiff
        outs[at][2] = prev_stiff
        at += 1
    if handoff:
        at += 1 if split else 0
        (p0, v0), (p1, v1) = results
        diff_p = [p1[i] - p0[i] for i in range(n)]
        diff_v = [[v1[i][c] - v0[i][c] for c in range(3)] for i in range(n)]
        for b, (pres, vel) in enumerate(((p0, v0), (diff_p, diff_v))):
            write_messages(b, messages(pres, vel, k_ref, m_ref, handoff[b]), outs[at], outs[at + 1])


def planes(count, like):
    return jax.ShapeDtypeStruct((count,) + like.shape[-2:], like.dtype)


def diagonal(x, by):
    spaces, groups = lax.axis_size("space"), lax.axis_size("tm")
    pairs = [
        (s * groups + c, (s + by) * groups + c + 1)
        for s in range(spaces)
        for c in range(groups - 1)
        if 0 <= s + by < spaces
    ]
    return lax.ppermute(x, ("space", "tm"), pairs)


def advance(states, sources, to_right, to_left, stiffness, inv_mass, consts, sizes, counts,
            next_count, split=False, finish=None, handoff=None, received=None, offset=0):
    if received is None:
        from_left = from_behind(to_right, "space", 1)
        from_right = from_behind(to_left, "space", -1)
    else:
        from_left, from_right = received
    first = consts is None
    if first:
        consts = from_left
    n = stiffness.shape[0]
    args = list(states) + [stiffness, inv_mass, consts, from_left, from_right]
    vmem = pl.BlockSpec(memory_space=pltpu.VMEM)
    specs = [vmem] * len(args)
    if finish is not None:
        flat = jax.ShapeDtypeStruct((1,) + stiffness.shape, stiffness.dtype)
        vflat = jax.ShapeDtypeStruct((1, 3) + stiffness.shape, stiffness.dtype)
        outs = [flat, vflat, flat, vflat]
        args += list(finish)
        specs += [pl.BlockSpec(memory_space=pltpu.SMEM), vmem, vmem]
    else:
        outs = [jax.ShapeDtypeStruct((len(sizes), 4) + stiffness.shape, stiffness.dtype)]
        if next_count:
            outs += [planes(2 * next_count, stiffness), planes(2 * next_count, stiffness)]
        if first:
            outs.append(planes(3, stiffness))
        if split:
            outs.append(jax.ShapeDtypeStruct((4,) + stiffness.shape, stiffness.dtype))
        if handoff:
            outs += [planes(4, stiffness), planes(4, stiffness)]
    kernel = functools.partial(
        pair_kernel, tuple(sizes), tuple(counts), tuple(sources), len(states), next_count, first,
        split, finish is not None, handoff, offset,
    )
    return pl.pallas_call(
        kernel, out_shape=tuple(outs), in_specs=specs, compiler_params=PARAMS
    )(*args)


def messages_kernel(sizes, sources, n_states, extras, *refs):
    states = refs[:n_states]
    k_ref, m_ref, right_out, left_out = refs[n_states:]
    n = k_ref.shape[0]
    for b, h in enumerate(sizes):
        pres, vel = read_slot(sources[b], states, n)
        write_messages(b, messages(pres, vel, k_ref, m_ref, h), right_out, left_out)
    if extras:
        width = 2 * len(sizes)
        right_out[width] = k_ref[n - 1]
        left_out[width] = m_ref[0]
        left_out[width + 1] = k_ref[0]


def first_messages(states, sources, stiffness, inv_mass, sizes, extras=False):
    width = 2 * len(sizes)
    kernel = functools.partial(messages_kernel, tuple(sizes), tuple(sources), len(states), extras)
    return pl.pallas_call(
        kernel,
        compiler_params=PARAMS,
        out_shape=(planes(width + (1 if extras else 0), stiffness), planes(width + (2 if extras else 0), stiffness)),
    )(*states, stiffness, inv_mass)


def coarse(carried, stiffness, inv_mass, consts):
    sources = (("flat", 0),)
    to_right, to_left = first_messages((carried,), sources, stiffness, inv_mass, (DT_COARSE,))
    (out,) = advance((carried,), sources, to_right, to_left, stiffness, inv_mass, consts,
                     (DT_COARSE,), (1,), 0)
    return out[0]


def on_device(
    guess_pressure, guess_velocity, initial_pressure, initial_velocity, stiffness, inv_mass
):
    fine_size = DT_COARSE / STEPS
    groups = lax.axis_size("tm")
    group = lax.axis_index("tm")
    assert stiffness.shape[0] >= 2 and STEPS % 2 == 0
    rounds = STEPS // 2
    fine2 = (fine_size, fine_size)

    inputs = (guess_pressure, guess_velocity, initial_pressure, initial_velocity)
    sources = (("input", 0, 1, True), ("input", 2, 3, False))
    to_right, to_left = first_messages(inputs, sources, stiffness, inv_mass, fine2, extras=True)
    state, to_right, to_left, consts = advance(
        inputs, sources, to_right, to_left, stiffness, inv_mass, None, fine2, (2, 2), 2,
    )
    packed = (("packed", 0, 0), ("packed", 0, 1))
    for repeat in range(1, rounds):
        count = 2 if repeat + 1 < rounds else 0
        last_round = repeat + 1 == rounds
        outs = advance(
            (state,), packed, to_right, to_left, stiffness, inv_mass, consts, fine2, (2, 2), count,
            split=last_round, handoff=(fine_size, DT_COARSE) if last_round else None,
        )
        state = outs[0]
        if count:
            to_right, to_left = outs[1], outs[2]
    relaxed, hand_right, hand_left = outs[-3], outs[-2], outs[-1]

    got = from_behind(relaxed, "tm", 1)
    received = (diagonal(hand_right, 1), diagonal(hand_left, -1))
    late_states = (got, state)
    late_sources = (("flat", 0), ("diff", 1, 1, 0))
    flag = jnp.reshape(group, (1,)).astype(jnp.int32)
    (moved,) = advance(late_states, (late_sources[1],), None, None, stiffness, inv_mass, consts,
                       (DT_COARSE,), (1,), 0, received=received, offset=1)
    late = None
    for repeat in range(rounds):
        count = 1 if repeat + 1 < rounds else 0
        if repeat == 0:
            states, srcs = late_states, late_sources[:1]
        else:
            states, srcs = (late,), (("packed", 0, 0),)
        finish = (flag, state, moved) if (groups == 2 and repeat + 1 == rounds) else None
        outs = advance(states, srcs, to_right, to_left, stiffness, inv_mass, consts, (fine_size,),
                       (2,), count, finish=finish, received=received if repeat == 0 else None)
        if finish is not None:
            return outs
        late = outs[0]
        if count:
            to_right, to_left = outs[1], outs[2]

    end = jnp.where(group == 0, state[1], late[0])
    resid = end - relaxed
    error, carried = resid, resid
    for repeat in range(groups - 1):
        carried = from_behind(carried, "tm", 1)
        carried = coarse(carried, stiffness, inv_mass, consts)
        error = error + carried
    corrected = relaxed + error
    return (corrected[0][None], corrected[1:][None], resid[0][None], resid[1:][None])


def solution(mesh):
    placed = (
        P("tm", "space", None, None),
        P("tm", None, "space", None, None),
        P("space", None, None),
        P(None, "space", None, None),
        P("space", None, None),
        P("space", None, None),
    )
    return jax.shard_map(
        on_device,
        mesh=mesh,
        in_specs=placed,
        out_specs=(
            P("tm", "space", None, None),
            P("tm", None, "space", None, None),
            P("tm", "space", None, None),
            P("tm", None, "space", None, None),
        ),
        check_vma=False,
    )
```
